32 devices in a mesh: group: 2 (over y), sub: 4 (over z), tile: 2 (over x), rep: 2 (over core).
Axes of the slice: x: 2, y: 2, z: 4, core: 2. Of those that a mesh axis runs over, the one named last changes fastest.
Arguments:
- right_side: bfloat16 [16, 1024, 512], P(('group', 'sub', 'tile'), None, 'rep'), parts along dimension 0, may hold values from -6 to 6
- interface_inverse: bfloat16 [16, 1024, 1024], P(('group', 'sub', 'tile')), parts along dimension 0, may hold values from -0.1875 to 0.1875
- coupling: float32 [16, 2, 128], P(('group', 'sub', 'tile')), parts along dimension 0, may hold values from 0.5 to 2
- trace_rows: int32 [16, 2, 128], P(('group', 'sub', 'tile')), parts along dimension 0, may hold values from 0 to 1023
- deflation_basis: bfloat16 [16, 1024, 128], P(('group', 'sub', 'tile')), parts along dimension 0, may hold values from -0.375 to 0.375
- deflation_counts: int32 [16], P(('group', 'sub', 'tile')), parts along dimension 0, may hold values from 32 to 128, as said below
- coarse_inverse: bfloat16 [8, 2, 128, 4, 256], P('group', 'tile', 'rep', 'sub'), parts along dimension 0, may hold values from -0.25 to 0.25
Outputs:
- corrected_field: bfloat16 [16, 1024, 512], P(('group', 'sub', 'tile'), None, 'rep'), parts along dimension 0
The draws below stay inside these ranges and needn't reach their ends.
There are 2 independent parts, one for each index of `group`. The reference program is written for one: setup_inputs(seed, part) draws one part's arguments, and reference() takes and returns one part's arrays. A program takes and returns all parts, laid end to end along the dimension named above; each array names one. Nothing has to cross between parts.
Inputs may be any that keep to these rules, and one draw needn't show every extreme that they name: `deflation_counts`: some subdomain has exactly 128 live deflation vectors.
All inputs are finite; a program needn't handle non-finite values.
Results may differ from the reference program's by a relative error of at most 0.035.
Values may be sent and summed in bfloat16 or wider, within the bound.
No kernel may reach another device: no remote copies, remote signals or barrier semaphores. Data moves between devices by JAX's collectives and lax.ppermute only.
A program may use at most 64 MiB of HBM per device.

```python
import jax
import jax.numpy as jnp
from jax import lax

IFACE_ROWS = 1024
FACE_ROWS = 128
DEFL_SLOTS = 128
ROUNDS = 2
SUBDOMAINS = 8
ALL_MODES = 512
COARSE_ORDER = 1024
N_SUB = 4
N_TILE = 2


def draw_deflation_counts(key, part):
    key_counts, key_fullest = jax.random.split(jax.random.fold_in(key, 11))
    counts = jax.random.randint(key_counts, (SUBDOMAINS,), DEFL_SLOTS // 4, DEFL_SLOTS + 1, dtype=jnp.int32)
    fullest = jax.random.randint(key_fullest, (), 0, SUBDOMAINS, dtype=jnp.int32)
    positions = jnp.arange(SUBDOMAINS, dtype=jnp.int32)
    return jnp.where(positions == fullest, DEFL_SLOTS, counts).astype(jnp.int32)


def touch_ends(values, rng, low, largest):
    dims = values.shape
    spot = [jax.random.randint(jax.random.fold_in(rng, axis), (), 0, dims[axis]) for axis in range(len(dims))]
    values = values.at[tuple(spot)].set(low)
    longest = dims.index(max(dims))
    spot[longest] = (spot[longest] + 1) % dims[longest]
    return values.at[tuple(spot)].set(largest)


def raised(entries, stream_key, source, target, parts, factor):
    def block_of(position):
        return (jnp.arange(entries.shape[position]) // (entries.shape[position] // parts)).reshape((-1,) + (1,) * (entries.ndim - 1 - position))

    one_side = jax.random.permutation(stream_key, parts)[block_of(target)]
    other_side = (block_of(target) + parts // 2) % parts
    return jnp.where((block_of(source) == one_side) | (block_of(source) == other_side), factor * entries, entries)


def level_of(stream_key, dims, cuts, low, largest):
    def one(axis_at, shards_of):
        heights = jax.random.uniform(jax.random.fold_in(jax.random.fold_in(stream_key, 6), axis_at), (shards_of,), jnp.float32, low / len(cuts), largest / len(cuts))
        return jnp.repeat(jnp.exp(heights), dims[axis_at] // shards_of).reshape((-1,) + (1,) * (len(dims) - axis_at - 1))

    loudness = one(*cuts[0])
    for cut in cuts[1:]:
        loudness = loudness * one(*cut)
    return loudness


def gaussian(rng, extent, scale, limit, cuts=(), kind=jnp.bfloat16):
    entries = scale * jax.random.normal(rng, extent, jnp.float32)
    if cuts:
        entries = entries * level_of(rng, extent, cuts, -0.22, 0.18)
    return jnp.clip(entries, -limit, limit).astype(kind)


def bell_draw_with(rng, dims, deviation, reach, shards, heavy, kind=jnp.bfloat16):
    array = deviation * jax.random.normal(rng, dims, jnp.float32)
    if shards:
        array = array * level_of(rng, dims, shards, -0.22, 0.18)
    return jnp.clip(raised(array, jax.random.fold_in(rng, 3), *heavy), -reach, reach).astype(kind)


def setup_inputs(seed: int = 0, part: int = 0) -> dict:
    key_list = jax.random.split(jax.random.key(seed), 8)
    part_splits = jax.random.split(jax.random.fold_in(key_list[7], part), 8)
    return {
        "right_side": gaussian(part_splits[0], (SUBDOMAINS, IFACE_ROWS, ALL_MODES), 1.0, 6.0, ((0, 8), (2, 2))),
        "interface_inverse": gaussian(part_splits[1], (SUBDOMAINS, IFACE_ROWS, IFACE_ROWS), IFACE_ROWS ** -0.5, 0.1875, ((0, 8),)),
        "coupling": jnp.clip(0.5 + 1.5 * jax.random.uniform(part_splits[2], (SUBDOMAINS, 2, FACE_ROWS), jnp.float32) ** level_of(part_splits[2], (SUBDOMAINS, 2, FACE_ROWS), ((0, 8),), -0.2, 0.2), 0.5, 2.0),
        "trace_rows": touch_ends(jax.random.randint(part_splits[3], (SUBDOMAINS, 2, FACE_ROWS), 0, IFACE_ROWS), jax.random.fold_in(part_splits[3], 1), 0, IFACE_ROWS - 1).astype(jnp.int32),
        "deflation_basis": gaussian(part_splits[4], (SUBDOMAINS, IFACE_ROWS, DEFL_SLOTS), (IFACE_ROWS // 4) ** -0.5, 0.375, ((0, 8),)),
        "deflation_counts": draw_deflation_counts(jax.random.fold_in(jax.random.fold_in(key_list[7], part), 71), part),
        "coarse_inverse": bell_draw_with(part_splits[6], (N_SUB, N_TILE, DEFL_SLOTS, N_SUB, N_TILE * DEFL_SLOTS), COARSE_ORDER ** -0.5, 0.25, ((1, 2), (2, 2), (3, 4)), (3, 0, 4, 2.0)),
    }


def batched_product(left_stack, right_stack):
    return lax.map(lambda operands: jnp.dot(operands[0], operands[1], preferred_element_type=jnp.float32), (left_stack, right_stack))


def reference(right_side, interface_inverse, coupling, trace_rows, deflation_basis, deflation_counts, coarse_inverse):
    slot_ids = jnp.arange(DEFL_SLOTS, dtype=jnp.int32)
    live_slots = slot_ids[None, :] < deflation_counts[:, None]
    masked_basis = jnp.where(live_slots[:, None, :], deflation_basis, jnp.zeros((), deflation_basis.dtype))
    basis_rows = jnp.swapaxes(masked_basis, 1, 2)
    coarse_columns = coarse_inverse.reshape(COARSE_ORDER, N_SUB, N_TILE * DEFL_SLOTS)
    source = right_side.astype(jnp.float32)
    iterate = jnp.zeros((SUBDOMAINS, IFACE_ROWS, ALL_MODES), jnp.float32)
    zero_face = jnp.zeros((1, FACE_ROWS, ALL_MODES), jnp.float32)
    for cycle_index in range(ROUNDS):
        lower_trace = jnp.take_along_axis(iterate, trace_rows[:, 0, :, None], axis=1)
        upper_trace = jnp.take_along_axis(iterate, trace_rows[:, 1, :, None], axis=1)
        from_lower = jnp.concatenate([zero_face, upper_trace[:-1]], axis=0)
        from_upper = jnp.concatenate([lower_trace[1:], zero_face], axis=0)
        lower_rows = source[:, :FACE_ROWS] + coupling[:, 0, :, None] * from_lower
        upper_rows = source[:, IFACE_ROWS - FACE_ROWS:] + coupling[:, 1, :, None] * from_upper
        boundary = jnp.concatenate([lower_rows, source[:, FACE_ROWS:IFACE_ROWS - FACE_ROWS], upper_rows], axis=1).astype(jnp.bfloat16)
        local_solve = batched_product(interface_inverse, boundary)
        defect = (local_solve - iterate).astype(jnp.bfloat16)
        projected = batched_product(basis_rows, defect).astype(jnp.bfloat16)
        vector = projected.reshape(N_SUB, N_TILE * DEFL_SLOTS, ALL_MODES)

        def add_part(total, index):
            columns = lax.dynamic_index_in_dim(coarse_columns, index, 1, keepdims=False)
            inputs = lax.dynamic_index_in_dim(vector, index, 0, keepdims=False)
            part = jnp.dot(columns, inputs, preferred_element_type=jnp.float32).astype(jnp.bfloat16)
            part = lax.optimization_barrier(part)
            return total + part.astype(jnp.float32), None

        start_total = jnp.zeros((COARSE_ORDER, ALL_MODES), jnp.float32)
        total, unused = lax.scan(add_part, start_total, jnp.arange(N_SUB, dtype=jnp.int32))
        coarse = total.astype(jnp.bfloat16).reshape(SUBDOMAINS, DEFL_SLOTS, ALL_MODES)
        iterate = local_solve + batched_product(masked_basis, coarse)
    return iterate.astype(jnp.bfloat16)
```

```python
import jax
import jax.numpy as jnp
from jax import lax
from jax.sharding import PartitionSpec as P

ROUNDS = 2
DUCT = ("sub", "tile")


def passed_along(shard, by):
    peers = lax.axis_size(DUCT)
    pairs = [(i, i + by) for i in range(peers) if 0 <= i + by < peers]
    return lax.ppermute(shard, DUCT, pairs)


def own_coarse_rows(coarse_inverse):
    rows = lax.all_to_all(coarse_inverse, "sub", split_axis=0, concat_axis=3, tiled=True)
    rows = lax.all_gather(rows, "rep", axis=2, tiled=True)
    return rows.reshape(rows.shape[2], rows.shape[3] * rows.shape[4])


def local(
    right_side,
    interface_inverse,
    coupling,
    trace_rows,
    deflation_basis,
    deflation_counts,
    coarse_inverse,
):
    source = right_side[0]
    inverse = interface_inverse[0]
    iface_rows = inverse.shape[0]
    face_rows = coupling.shape[2]
    slot_count = deflation_basis.shape[2]
    slot_ids = jnp.arange(slot_count, dtype=jnp.int32)
    masked_basis = jnp.where(
        slot_ids[None, :] < deflation_counts[0],
        deflation_basis[0],
        jnp.zeros((), deflation_basis.dtype),
    )
    coarse_rows = own_coarse_rows(coarse_inverse)
    lower_gain = coupling[0, 0][:, None]
    upper_gain = coupling[0, 1][:, None]

    def coarse_step(local_solve, defect):
        projected = lax.dot_general(
            masked_basis, defect, (((0,), (0,)), ((), ())), preferred_element_type=jnp.float32
        ).astype(jnp.bfloat16)
        vector = lax.all_gather(projected, DUCT, axis=0, tiled=True)
        coarse = jnp.dot(coarse_rows, vector, preferred_element_type=jnp.float32).astype(
            jnp.bfloat16
        )
        return local_solve + jnp.dot(masked_basis, coarse, preferred_element_type=jnp.float32)

    local_solve = jnp.dot(inverse, source, preferred_element_type=jnp.float32)
    iterate = coarse_step(local_solve, local_solve.astype(jnp.bfloat16))
    for cycle_index in range(1, ROUNDS):
        lower_trace = iterate[trace_rows[0, 0]]
        upper_trace = iterate[trace_rows[0, 1]]
        from_lower = passed_along(upper_trace.astype(jnp.bfloat16), 1).astype(jnp.float32)
        from_upper = passed_along(lower_trace.astype(jnp.bfloat16), -1).astype(jnp.float32)
        lower_rows = source[:face_rows].astype(jnp.float32) + lower_gain * from_lower
        upper_rows = source[iface_rows - face_rows :].astype(jnp.float32) + upper_gain * from_upper
        boundary = jnp.concatenate(
            [
                lower_rows.astype(jnp.bfloat16),
                source[face_rows : iface_rows - face_rows],
                upper_rows.astype(jnp.bfloat16),
            ],
            axis=0,
        )
        local_solve = jnp.dot(inverse, boundary, preferred_element_type=jnp.float32)
        iterate = coarse_step(local_solve, (local_solve - iterate).astype(jnp.bfloat16))
    return iterate.astype(jnp.bfloat16)[None]


def solution(mesh):
    placed = (
        P(("group", "sub", "tile"), None, "rep"),
        P(("group", "sub", "tile"), None, None),
        P(("group", "sub", "tile"), None, None),
        P(("group", "sub", "tile"), None, None),
        P(("group", "sub", "tile"), None, None),
        P(("group", "sub", "tile")),
        P("group", "tile", "rep", "sub", None),
    )
    return jax.shard_map(
        local,
        mesh=mesh,
        in_specs=placed,
        out_specs=P(("group", "sub", "tile"), None, "rep"),
        check_vma=False,
    )
```

```python
import jax
import jax.numpy as jnp
from jax import lax
from jax.sharding import PartitionSpec as P

ROUNDS = 2
DUCT = ("sub", "tile")
OWNERS = ("sub", "rep")
MAX_RING = 8


def passed_along(shard, by):
    peers = lax.axis_size(DUCT)
    pairs = [(i, i + by) for i in range(peers) if 0 <= i + by < peers]
    return lax.ppermute(shard, DUCT, pairs)


def shifted_copies(pick, axes):
    peers = lax.axis_size(axes)
    parts = [pick(0)]
    for k in range(1, peers):
        parts.append(lax.ppermute(pick(k), axes, [(i, (i + k) % peers) for i in range(peers)]))
    return jnp.stack(parts)


def sources(axes):
    peers = lax.axis_size(axes)
    return (lax.axis_index(axes) - jnp.arange(peers)) % peers


def own_coarse_rows(coarse_inverse):
    out_sub, _, half_slots, _, in_cols = coarse_inverse.shape
    if lax.axis_size(OWNERS) > MAX_RING:
        rows = lax.all_to_all(coarse_inverse, "sub", split_axis=0, concat_axis=3, tiled=True)
        rows = lax.all_gather(rows, "rep", axis=2, tiled=True)
        return rows.reshape(rows.shape[2], rows.shape[3] * rows.shape[4])
    reps = lax.axis_size("rep")
    blocks = coarse_inverse[:, 0, :, 0, :]

    def pick(k):
        target = (lax.axis_index(OWNERS) + k) % lax.axis_size(OWNERS)
        return lax.dynamic_index_in_dim(blocks, target // reps, 0, keepdims=False)

    parts = shifted_copies(pick, OWNERS)
    order = jnp.argsort(sources(OWNERS))
    parts = jnp.take(parts, order, axis=0)
    parts = parts.reshape(out_sub, reps, half_slots, in_cols).transpose(1, 2, 0, 3)
    return parts.reshape(reps * half_slots, out_sub * in_cols)


def gathered_product(coarse_rows, projected):
    peers = lax.axis_size(DUCT)
    if peers > MAX_RING:
        vector = lax.all_gather(projected, DUCT, axis=0, tiled=True)
        return jnp.dot(coarse_rows, vector, preferred_element_type=jnp.float32)
    parts = shifted_copies(lambda k: projected, DUCT)
    return jnp.dot(
        coarse_rows, parts.reshape(-1, parts.shape[-1]), preferred_element_type=jnp.float32
    )


def local(
    right_side,
    interface_inverse,
    coupling,
    trace_rows,
    deflation_basis,
    deflation_counts,
    coarse_inverse,
):
    source = right_side[0]
    inverse = interface_inverse[0]
    iface_rows = inverse.shape[0]
    face_rows = coupling.shape[2]
    slot_count = deflation_basis.shape[2]
    slot_ids = jnp.arange(slot_count, dtype=jnp.int32)
    masked_basis = jnp.where(
        slot_ids[None, :] < deflation_counts[0],
        deflation_basis[0],
        jnp.zeros((), deflation_basis.dtype),
    )
    coarse_rows = own_coarse_rows(coarse_inverse)
    peers = lax.axis_size(DUCT)
    if peers <= MAX_RING:
        coarse_rows = jnp.take(
            coarse_rows.reshape(coarse_rows.shape[0], peers, -1), sources(DUCT), axis=1
        ).reshape(coarse_rows.shape[0], -1)
    lower_gain = coupling[0, 0][:, None]
    upper_gain = coupling[0, 1][:, None]

    def coarse_step(local_solve, defect):
        projected = lax.dot_general(
            masked_basis, defect, (((0,), (0,)), ((), ())), preferred_element_type=jnp.float32
        ).astype(jnp.bfloat16)
        coarse = gathered_product(coarse_rows, projected).astype(jnp.bfloat16)
        return local_solve + jnp.dot(masked_basis, coarse, preferred_element_type=jnp.float32)

    local_solve = jnp.dot(inverse, source, preferred_element_type=jnp.float32)
    iterate = coarse_step(local_solve, local_solve.astype(jnp.bfloat16))
    for cycle_index in range(1, ROUNDS):
        lower_trace = iterate[trace_rows[0, 0]]
        upper_trace = iterate[trace_rows[0, 1]]
        from_lower = passed_along(upper_trace.astype(jnp.bfloat16), 1).astype(jnp.float32)
        from_upper = passed_along(lower_trace.astype(jnp.bfloat16), -1).astype(jnp.float32)
        lower_rows = source[:face_rows].astype(jnp.float32) + lower_gain * from_lower
        upper_rows = source[iface_rows - face_rows :].astype(jnp.float32) + upper_gain * from_upper
        boundary = jnp.concatenate(
            [
                lower_rows.astype(jnp.bfloat16),
                source[face_rows : iface_rows - face_rows],
                upper_rows.astype(jnp.bfloat16),
            ],
            axis=0,
        )
        local_solve = jnp.dot(inverse, boundary, preferred_element_type=jnp.float32)
        iterate = coarse_step(local_solve, (local_solve - iterate).astype(jnp.bfloat16))
    return iterate.astype(jnp.bfloat16)[None]


def solution(mesh):
    placed = (
        P(("group", "sub", "tile"), None, "rep"),
        P(("group", "sub", "tile"), None, None),
        P(("group", "sub", "tile"), None, None),
        P(("group", "sub", "tile"), None, None),
        P(("group", "sub", "tile"), None, None),
        P(("group", "sub", "tile")),
        P("group", "tile", "rep", "sub", None),
    )
    return jax.shard_map(
        local,
        mesh=mesh,
        in_specs=placed,
        out_specs=P(("group", "sub", "tile"), None, "rep"),
        check_vma=False,
    )
```

```python
import jax
import jax.numpy as jnp
from jax import lax
from jax.sharding import PartitionSpec as P

ROUNDS = 2
DUCT = ("sub", "tile")
MAX_RING = 8


def passed_along(shard, by):
    peers = lax.axis_size(DUCT)
    pairs = [(i, i + by) for i in range(peers) if 0 <= i + by < peers]
    return lax.ppermute(shard, DUCT, pairs)


def own_coarse_rows(coarse_inverse):
    rows = lax.all_to_all(coarse_inverse, "sub", split_axis=0, concat_axis=3, tiled=True)
    rows = lax.all_gather(rows, "rep", axis=2, tiled=True)
    return rows.reshape(rows.shape[2], rows.shape[3] * rows.shape[4])


def gathered(projected, up_trace, low_trace):
    peers = lax.axis_size(DUCT)
    rows = projected.shape[0]
    if peers > MAX_RING:
        vector = lax.all_gather(projected, DUCT, axis=0, tiled=True)
        if up_trace is None:
            return vector, None, None
        return vector, passed_along(up_trace, 1), passed_along(low_trace, -1)
    parts = [projected]
    extras = {}
    if up_trace is not None:
        extras.setdefault(1, []).append(up_trace)
        extras.setdefault(peers - 1, []).append(low_trace)
    came = {}
    for k in range(1, peers):
        piece = jnp.concatenate([projected] + extras.get(k, []), axis=0)
        got = lax.ppermute(piece, DUCT, [(i, (i + k) % peers) for i in range(peers)])
        parts.append(got[:rows])
        came[k] = got[rows:]
    vector = jnp.concatenate(parts, axis=0)
    if up_trace is None:
        return vector, None, None
    from_lower = came[1][: up_trace.shape[0]]
    from_upper = came[peers - 1][came[peers - 1].shape[0] - low_trace.shape[0] :]
    return vector, from_lower, from_upper


def block_order(matrix):
    peers = lax.axis_size(DUCT)
    if peers > MAX_RING:
        return matrix
    came_from = (lax.axis_index(DUCT) - jnp.arange(peers)) % peers
    blocks = matrix.reshape(matrix.shape[0], peers, -1)
    return jnp.take(blocks, came_from, axis=1).reshape(matrix.shape)


def local(
    right_side,
    interface_inverse,
    coupling,
    trace_rows,
    deflation_basis,
    deflation_counts,
    coarse_inverse,
):
    source = right_side[0]
    inverse = interface_inverse[0]
    iface_rows = inverse.shape[0]
    face_rows = coupling.shape[2]
    slot_count = deflation_basis.shape[2]
    peers = lax.axis_size(DUCT)
    position = lax.axis_index(DUCT)
    slot_ids = jnp.arange(slot_count, dtype=jnp.int32)
    masked_basis = jnp.where(
        slot_ids[None, :] < deflation_counts[0],
        deflation_basis[0],
        jnp.zeros((), deflation_basis.dtype),
    )
    lower_rows_at = trace_rows[0, 0]
    upper_rows_at = trace_rows[0, 1]
    coarse_rows = own_coarse_rows(coarse_inverse)
    width = coarse_rows.shape[1]
    below = passed_along(jnp.concatenate([coarse_rows, masked_basis[upper_rows_at]], axis=1), 1)
    above = passed_along(jnp.concatenate([coarse_rows, masked_basis[lower_rows_at]], axis=1), -1)
    coarse_all = block_order(
        jnp.concatenate([coarse_rows, below[:, :width], above[:, :width]], axis=0)
    )
    below_basis = below[:, width:]
    above_basis = above[:, width:]
    has_lower = position > 0
    has_upper = position < peers - 1
    lower_gain = coupling[0, 0][:, None]
    upper_gain = coupling[0, 1][:, None]
    block = coarse_rows.shape[0]

    iterate = None
    boundary = source
    for cycle_index in range(ROUNDS):
        local_solve = jnp.dot(inverse, boundary, preferred_element_type=jnp.float32)
        if iterate is None:
            defect = local_solve.astype(jnp.bfloat16)
        else:
            defect = (local_solve - iterate).astype(jnp.bfloat16)
        projected = lax.dot_general(
            masked_basis, defect, (((0,), (0,)), ((), ())), preferred_element_type=jnp.float32
        ).astype(jnp.bfloat16)
        last = cycle_index == ROUNDS - 1
        if last:
            vector = gathered(projected, None, None)[0]
            coarse = jnp.dot(coarse_all[:block], vector, preferred_element_type=jnp.float32)
            coarse = coarse.astype(jnp.bfloat16)
            iterate = local_solve + jnp.dot(masked_basis, coarse, preferred_element_type=jnp.float32)
            break
        vector, solve_lower, solve_upper = gathered(
            projected,
            local_solve[upper_rows_at].astype(jnp.bfloat16),
            local_solve[lower_rows_at].astype(jnp.bfloat16),
        )
        coarse = jnp.dot(coarse_all, vector, preferred_element_type=jnp.float32).astype(
            jnp.bfloat16
        )
        iterate = local_solve + jnp.dot(
            masked_basis, coarse[:block], preferred_element_type=jnp.float32
        )
        from_lower = solve_lower.astype(jnp.float32) + jnp.dot(
            below_basis, coarse[block : 2 * block], preferred_element_type=jnp.float32
        )
        from_upper = solve_upper.astype(jnp.float32) + jnp.dot(
            above_basis, coarse[2 * block :], preferred_element_type=jnp.float32
        )
        from_lower = jnp.where(has_lower, from_lower, 0.0)
        from_upper = jnp.where(has_upper, from_upper, 0.0)
        lower_rows = source[:face_rows].astype(jnp.float32) + lower_gain * from_lower
        upper_rows = source[iface_rows - face_rows :].astype(jnp.float32) + upper_gain * from_upper
        boundary = jnp.concatenate(
            [
                lower_rows.astype(jnp.bfloat16),
                source[face_rows : iface_rows - face_rows],
                upper_rows.astype(jnp.bfloat16),
            ],
            axis=0,
        )
    return iterate.astype(jnp.bfloat16)[None]


def solution(mesh):
    placed = (
        P(("group", "sub", "tile"), None, "rep"),
        P(("group", "sub", "tile"), None, None),
        P(("group", "sub", "tile"), None, None),
        P(("group", "sub", "tile"), None, None),
        P(("group", "sub", "tile"), None, None),
        P(("group", "sub", "tile")),
        P("group", "tile", "rep", "sub", None),
    )
    return jax.shard_map(
        local,
        mesh=mesh,
        in_specs=placed,
        out_specs=P(("group", "sub", "tile"), None, "rep"),
        check_vma=False,
    )
```

```python
import jax
import jax.numpy as jnp
from jax import lax
from jax.sharding import PartitionSpec as P

ROUNDS = 2
DUCT = ("sub", "tile")


def passed_along(shard, by):
    peers = lax.axis_size(DUCT)
    pairs = [(i, i + by) for i in range(peers) if 0 <= i + by < peers]
    return lax.ppermute(shard, DUCT, pairs)


def swapped(shard, axis):
    return lax.ppermute(shard, axis, [(0, 1), (1, 0)])


def gathered(shard, axis, dim):
    if lax.axis_size(axis) != 2:
        return lax.all_gather(shard, axis, axis=dim, tiled=True)
    other = swapped(shard, axis)
    first = lax.axis_index(axis) == 0
    return jnp.concatenate(
        [jnp.where(first, shard, other), jnp.where(first, other, shard)], axis=dim
    )


def local(
    right_side,
    interface_inverse,
    coupling,
    trace_rows,
    deflation_basis,
    deflation_counts,
    coarse_inverse,
):
    source = right_side[0]
    inverse = interface_inverse[0]
    iface_rows = inverse.shape[0]
    face_rows = coupling.shape[2]
    slot_count = deflation_basis.shape[2]
    sub_count = lax.axis_size("sub")
    sub_index = lax.axis_index("sub")
    slot_ids = jnp.arange(slot_count, dtype=jnp.int32)
    masked_basis = jnp.where(
        slot_ids[None, :] < deflation_counts[0],
        deflation_basis[0],
        jnp.zeros((), deflation_basis.dtype),
    )
    half_block = coarse_inverse[:, 0, :, 0, :]
    columns = gathered(half_block, "rep", 1)
    lower_gain = coupling[0, 0][:, None]
    upper_gain = coupling[0, 1][:, None]

    def coarse_step(local_solve, defect):
        projected = lax.dot_general(
            masked_basis, defect, (((0,), (0,)), ((), ())), preferred_element_type=jnp.float32
        ).astype(jnp.bfloat16)
        inputs = gathered(projected, "tile", 0)
        partial = jnp.einsum(
            "jsc,cm->jsm", columns, inputs, preferred_element_type=jnp.float32
        ).astype(jnp.bfloat16)
        total = lax.dynamic_index_in_dim(partial, sub_index, 0, keepdims=False).astype(
            jnp.float32
        )
        for k in range(1, sub_count):
            piece = lax.dynamic_index_in_dim(partial, (sub_index + k) % sub_count, 0, keepdims=False)
            total = total + lax.ppermute(
                piece, "sub", [(i, (i + k) % sub_count) for i in range(sub_count)]
            ).astype(jnp.float32)
        coarse = total.astype(jnp.bfloat16)
        return local_solve + jnp.dot(masked_basis, coarse, preferred_element_type=jnp.float32)

    local_solve = jnp.dot(inverse, source, preferred_element_type=jnp.float32)
    iterate = coarse_step(local_solve, local_solve.astype(jnp.bfloat16))
    for cycle_index in range(1, ROUNDS):
        lower_trace = iterate[trace_rows[0, 0]]
        upper_trace = iterate[trace_rows[0, 1]]
        from_lower = passed_along(upper_trace.astype(jnp.bfloat16), 1).astype(jnp.float32)
        from_upper = passed_along(lower_trace.astype(jnp.bfloat16), -1).astype(jnp.float32)
        lower_rows = source[:face_rows].astype(jnp.float32) + lower_gain * from_lower
        upper_rows = source[iface_rows - face_rows :].astype(jnp.float32) + upper_gain * from_upper
        boundary = jnp.concatenate(
            [
                lower_rows.astype(jnp.bfloat16),
                source[face_rows : iface_rows - face_rows],
                upper_rows.astype(jnp.bfloat16),
            ],
            axis=0,
        )
        local_solve = jnp.dot(inverse, boundary, preferred_element_type=jnp.float32)
        iterate = coarse_step(local_solve, (local_solve - iterate).astype(jnp.bfloat16))
    return iterate.astype(jnp.bfloat16)[None]


def solution(mesh):
    placed = (
        P(("group", "sub", "tile"), None, "rep"),
        P(("group", "sub", "tile"), None, None),
        P(("group", "sub", "tile"), None, None),
        P(("group", "sub", "tile"), None, None),
        P(("group", "sub", "tile"), None, None),
        P(("group", "sub", "tile")),
        P("group", "tile", "rep", "sub", None),
    )
    return jax.shard_map(
        local,
        mesh=mesh,
        in_specs=placed,
        out_specs=P(("group", "sub", "tile"), None, "rep"),
        check_vma=False,
    )
```

```python
import jax
import jax.numpy as jnp
from jax import lax
from jax.sharding import PartitionSpec as P

ROUNDS = 2
DUCT = ("sub", "tile")


def passed_along(shard, by):
    peers = lax.axis_size(DUCT)
    pairs = [(i, i + by) for i in range(peers) if 0 <= i + by < peers]
    return lax.ppermute(shard, DUCT, pairs)


def swapped(shard, axis):
    return lax.ppermute(shard, axis, [(0, 1), (1, 0)])


def gathered(shard, axis, dim):
    if lax.axis_size(axis) != 2:
        return lax.all_gather(shard, axis, axis=dim, tiled=True)
    other = swapped(shard, axis)
    first = lax.axis_index(axis) == 0
    return jnp.concatenate(
        [jnp.where(first, shard, other), jnp.where(first, other, shard)], axis=dim
    )


def local(
    right_side,
    interface_inverse,
    coupling,
    trace_rows,
    deflation_basis,
    deflation_counts,
    coarse_inverse,
):
    source = right_side[0]
    inverse = interface_inverse[0]
    iface_rows = inverse.shape[0]
    face_rows = coupling.shape[2]
    slot_count = deflation_basis.shape[2]
    sub_count = lax.axis_size("sub")
    sub_index = lax.axis_index("sub")
    slot_ids = jnp.arange(slot_count, dtype=jnp.int32)
    masked_basis = jnp.where(
        slot_ids[None, :] < deflation_counts[0],
        deflation_basis[0],
        jnp.zeros((), deflation_basis.dtype),
    )
    half_block = coarse_inverse[:, 0, :, 0, :]
    columns = gathered(half_block, "rep", 1)
    lower_gain = coupling[0, 0][:, None]
    upper_gain = coupling[0, 1][:, None]

    lower_at = trace_rows[0, 0]
    upper_at = trace_rows[0, 1]
    lower_basis = masked_basis[lower_at]
    upper_basis = masked_basis[upper_at]
    face_inverse = jnp.concatenate(
        [inverse[:, :face_rows], inverse[:, iface_rows - face_rows :]], axis=1
    )

    def coarse_of(defect):
        projected = lax.dot_general(
            masked_basis, defect, (((0,), (0,)), ((), ())), preferred_element_type=jnp.float32
        ).astype(jnp.bfloat16)
        inputs = gathered(projected, "tile", 0)
        partial = jnp.einsum(
            "jsc,cm->jsm", columns, inputs, preferred_element_type=jnp.float32
        ).astype(jnp.bfloat16)
        total = lax.dynamic_index_in_dim(partial, sub_index, 0, keepdims=False).astype(
            jnp.float32
        )
        for k in range(1, sub_count):
            piece = lax.dynamic_index_in_dim(partial, (sub_index + k) % sub_count, 0, keepdims=False)
            total = total + lax.ppermute(
                piece, "sub", [(i, (i + k) % sub_count) for i in range(sub_count)]
            ).astype(jnp.float32)
        return total.astype(jnp.bfloat16)

    base_solve = jnp.dot(inverse, source, preferred_element_type=jnp.float32)
    local_solve = base_solve
    defect = local_solve.astype(jnp.bfloat16)
    earlier = None
    for cycle_index in range(ROUNDS):
        coarse = coarse_of(defect)
        correction = jnp.dot(masked_basis, coarse, preferred_element_type=jnp.float32)
        iterate = local_solve + correction
        if cycle_index == ROUNDS - 1:
            break
        lower_trace = local_solve[lower_at] + jnp.dot(
            lower_basis, coarse, preferred_element_type=jnp.float32
        )
        upper_trace = local_solve[upper_at] + jnp.dot(
            upper_basis, coarse, preferred_element_type=jnp.float32
        )
        from_lower = passed_along(upper_trace.astype(jnp.bfloat16), 1).astype(jnp.float32)
        from_upper = passed_along(lower_trace.astype(jnp.bfloat16), -1).astype(jnp.float32)
        faces = jnp.concatenate(
            [lower_gain * from_lower, upper_gain * from_upper], axis=0
        ).astype(jnp.bfloat16)
        change = jnp.dot(face_inverse, faces, preferred_element_type=jnp.float32)
        local_solve = base_solve + change
        step = change if earlier is None else change - earlier
        defect = (step - correction).astype(jnp.bfloat16)
        earlier = change
    return iterate.astype(jnp.bfloat16)[None]


def solution(mesh):
    placed = (
        P(("group", "sub", "tile"), None, "rep"),
        P(("group", "sub", "tile"), None, None),
        P(("group", "sub", "tile"), None, None),
        P(("group", "sub", "tile"), None, None),
        P(("group", "sub", "tile"), None, None),
        P(("group", "sub", "tile")),
        P("group", "tile", "rep", "sub", None),
    )
    return jax.shard_map(
        local,
        mesh=mesh,
        in_specs=placed,
        out_specs=P(("group", "sub", "tile"), None, "rep"),
        check_vma=False,
    )
```

```python
import jax
import jax.numpy as jnp
from jax import lax
from jax.sharding import PartitionSpec as P

ROUNDS = 2
DUCT = ("sub", "tile")


def passed_along(shard, by):
    peers = lax.axis_size(DUCT)
    pairs = [(i, i + by) for i in range(peers) if 0 <= i + by < peers]
    return lax.ppermute(shard, DUCT, pairs)


def swapped(shard, axis):
    return lax.ppermute(shard, axis, [(0, 1), (1, 0)])


def gathered(shard, axis, dim):
    if lax.axis_size(axis) != 2:
        return lax.all_gather(shard, axis, axis=dim, tiled=True)
    other = swapped(shard, axis)
    first = lax.axis_index(axis) == 0
    return jnp.concatenate(
        [jnp.where(first, shard, other), jnp.where(first, other, shard)], axis=dim
    )


def local(
    right_side,
    interface_inverse,
    coupling,
    trace_rows,
    deflation_basis,
    deflation_counts,
    coarse_inverse,
):
    source = right_side[0]
    inverse = interface_inverse[0]
    iface_rows = inverse.shape[0]
    face_rows = coupling.shape[2]
    slot_count = deflation_basis.shape[2]
    sub_count = lax.axis_size("sub")
    sub_index = lax.axis_index("sub")
    slot_ids = jnp.arange(slot_count, dtype=jnp.int32)
    masked_basis = jnp.where(
        slot_ids[None, :] < deflation_counts[0],
        deflation_basis[0],
        jnp.zeros((), deflation_basis.dtype),
    )
    half_block = coarse_inverse[:, 0, :, 0, :]
    columns = gathered(half_block, "rep", 1)
    lower_gain = coupling[0, 0][:, None]
    upper_gain = coupling[0, 1][:, None]

    lower_at = trace_rows[0, 0]
    upper_at = trace_rows[0, 1]
    lower_basis = masked_basis[lower_at]
    upper_basis = masked_basis[upper_at]
    face_inverse = jnp.concatenate(
        [inverse[:, :face_rows], inverse[:, iface_rows - face_rows :]], axis=1
    )

    def coarse_input(defect):
        return lax.dot_general(
            masked_basis, defect, (((0,), (0,)), ((), ())), preferred_element_type=jnp.float32
        ).astype(jnp.bfloat16)

    def coarse_of(inputs):
        partial = jnp.einsum(
            "jsc,cm->jsm", columns, inputs, preferred_element_type=jnp.float32
        ).astype(jnp.bfloat16)
        total = lax.dynamic_index_in_dim(partial, sub_index, 0, keepdims=False).astype(
            jnp.float32
        )
        for k in range(1, sub_count):
            piece = lax.dynamic_index_in_dim(partial, (sub_index + k) % sub_count, 0, keepdims=False)
            total = total + lax.ppermute(
                piece, "sub", [(i, (i + k) % sub_count) for i in range(sub_count)]
            ).astype(jnp.float32)
        return total.astype(jnp.bfloat16)

    pairwise = lax.axis_size("tile") == 2 and ROUNDS == 2
    tile_index = lax.axis_index("tile")
    gains = coupling[0]
    if pairwise:
        sends = jnp.dot(masked_basis.T, face_inverse, preferred_element_type=jnp.float32)
        keeps = jnp.dot(masked_basis.T, masked_basis, preferred_element_type=jnp.float32)
        mine = jnp.concatenate([sends, keeps], axis=1).astype(jnp.bfloat16)
        theirs = swapped(mine, "tile")
        partner_gains = swapped(gains, "tile")
        duct_pairs = []
        peers = lax.axis_size(DUCT)
        for i in range(peers):
            target = i - 2 if i % 2 == 0 else i + 2
            if 0 <= target < peers:
                duct_pairs.append((i, target))

    def projection_of(mix, faces, coarse):
        return (
            jnp.dot(mix[:, : faces.shape[0]], faces, preferred_element_type=jnp.float32)
            - jnp.dot(mix[:, faces.shape[0] :], coarse, preferred_element_type=jnp.float32)
        ).astype(jnp.bfloat16)

    def face_rows_of(gain, lower, upper):
        return jnp.concatenate(
            [gain[0][:, None] * lower, gain[1][:, None] * upper], axis=0
        ).astype(jnp.bfloat16)

    base_solve = jnp.dot(inverse, source, preferred_element_type=jnp.float32)
    local_solve = base_solve
    inputs = gathered(coarse_input(local_solve.astype(jnp.bfloat16)), "tile", 0)
    earlier = None
    for cycle_index in range(ROUNDS):
        coarse = coarse_of(inputs)
        correction = jnp.dot(masked_basis, coarse, preferred_element_type=jnp.float32)
        iterate = local_solve + correction
        if cycle_index == ROUNDS - 1:
            break
        lower_trace = (
            local_solve[lower_at] + jnp.dot(lower_basis, coarse, preferred_element_type=jnp.float32)
        ).astype(jnp.bfloat16)
        upper_trace = (
            local_solve[upper_at] + jnp.dot(upper_basis, coarse, preferred_element_type=jnp.float32)
        ).astype(jnp.bfloat16)
        rows = lower_trace.shape[0]
        if pairwise:
            got_lower = passed_along(jnp.concatenate([upper_trace, coarse], axis=0), 1)
            got_upper = passed_along(jnp.concatenate([lower_trace, coarse], axis=0), -1)
            crossing = lax.ppermute(
                jnp.where(tile_index == 0, lower_trace, upper_trace), DUCT, duct_pairs
            )
            from_lower = got_lower[:rows].astype(jnp.float32)
            from_upper = got_upper[:rows].astype(jnp.float32)
            faces = face_rows_of(gains, from_lower, from_upper)
            first = tile_index == 0
            partner_lower = jnp.where(first, upper_trace, crossing).astype(jnp.float32)
            partner_upper = jnp.where(first, crossing, lower_trace).astype(jnp.float32)
            partner_coarse = jnp.where(first, got_upper[rows:], got_lower[rows:])
            partner_faces = face_rows_of(partner_gains, partner_lower, partner_upper)
            own = projection_of(mine, faces, coarse)
            other = projection_of(theirs, partner_faces, partner_coarse)
            inputs = jnp.concatenate(
                [jnp.where(first, own, other), jnp.where(first, other, own)], axis=0
            )
        else:
            from_lower = passed_along(upper_trace, 1).astype(jnp.float32)
            from_upper = passed_along(lower_trace, -1).astype(jnp.float32)
            faces = face_rows_of(gains, from_lower, from_upper)
        change = jnp.dot(face_inverse, faces, preferred_element_type=jnp.float32)
        local_solve = base_solve + change
        if not pairwise:
            step = change if earlier is None else change - earlier
            inputs = gathered(coarse_input((step - correction).astype(jnp.bfloat16)), "tile", 0)
        earlier = change
    return iterate.astype(jnp.bfloat16)[None]


def solution(mesh):
    placed = (
        P(("group", "sub", "tile"), None, "rep"),
        P(("group", "sub", "tile"), None, None),
        P(("group", "sub", "tile"), None, None),
        P(("group", "sub", "tile"), None, None),
        P(("group", "sub", "tile"), None, None),
        P(("group", "sub", "tile")),
        P("group", "tile", "rep", "sub", None),
    )
    return jax.shard_map(
        local,
        mesh=mesh,
        in_specs=placed,
        out_specs=P(("group", "sub", "tile"), None, "rep"),
        check_vma=False,
    )
```

```python
import jax
import jax.numpy as jnp
from jax import lax
from jax.sharding import PartitionSpec as P

ROUNDS = 2
DUCT = ("sub", "tile")


def passed_along(shard, by):
    peers = lax.axis_size(DUCT)
    pairs = [(i, i + by) for i in range(peers) if 0 <= i + by < peers]
    return lax.ppermute(shard, DUCT, pairs)


def swapped(shard, axis):
    return lax.ppermute(shard, axis, [(0, 1), (1, 0)])


def gathered(shard, axis, dim):
    if lax.axis_size(axis) != 2:
        return lax.all_gather(shard, axis, axis=dim, tiled=True)
    other = swapped(shard, axis)
    first = lax.axis_index(axis) == 0
    return jnp.concatenate(
        [jnp.where(first, shard, other), jnp.where(first, other, shard)], axis=dim
    )


def local(
    right_side,
    interface_inverse,
    coupling,
    trace_rows,
    deflation_basis,
    deflation_counts,
    coarse_inverse,
):
    source = right_side[0]
    inverse = interface_inverse[0]
    iface_rows = inverse.shape[0]
    face_rows = coupling.shape[2]
    slot_count = deflation_basis.shape[2]
    sub_count = lax.axis_size("sub")
    sub_index = lax.axis_index("sub")
    slot_ids = jnp.arange(slot_count, dtype=jnp.int32)
    masked_basis = jnp.where(
        slot_ids[None, :] < deflation_counts[0],
        deflation_basis[0],
        jnp.zeros((), deflation_basis.dtype),
    )
    half_block = coarse_inverse[:, 0, :, 0, :]
    columns = gathered(half_block, "rep", 1)
    lower_gain = coupling[0, 0][:, None]
    upper_gain = coupling[0, 1][:, None]

    lower_at = trace_rows[0, 0]
    upper_at = trace_rows[0, 1]
    lower_basis = masked_basis[lower_at]
    upper_basis = masked_basis[upper_at]
    face_inverse = jnp.concatenate(
        [inverse[:, :face_rows], inverse[:, iface_rows - face_rows :]], axis=1
    )

    def coarse_input(defect):
        return lax.dot_general(
            masked_basis, defect, (((0,), (0,)), ((), ())), preferred_element_type=jnp.float32
        ).astype(jnp.bfloat16)

    def coarse_of(inputs):
        partial = jnp.einsum(
            "jsc,cm->jsm", columns, inputs, preferred_element_type=jnp.float32
        ).astype(jnp.bfloat16)
        total = lax.dynamic_index_in_dim(partial, sub_index, 0, keepdims=False).astype(
            jnp.float32
        )
        for k in range(1, sub_count):
            piece = lax.dynamic_index_in_dim(partial, (sub_index + k) % sub_count, 0, keepdims=False)
            total = total + lax.ppermute(
                piece, "sub", [(i, (i + k) % sub_count) for i in range(sub_count)]
            ).astype(jnp.float32)
        return total.astype(jnp.bfloat16)

    pairwise = lax.axis_size("tile") == 2 and ROUNDS == 2
    tile_index = lax.axis_index("tile")
    gains = coupling[0]
    if pairwise:
        sends = jnp.dot(masked_basis.T, face_inverse, preferred_element_type=jnp.float32)
        keeps = jnp.dot(masked_basis.T, masked_basis, preferred_element_type=jnp.float32)
        mine = jnp.concatenate([sends, keeps], axis=1).astype(jnp.bfloat16)
        gains_high = gains.T.astype(jnp.bfloat16)
        gains_low = (gains.T - gains_high.astype(jnp.float32)).astype(jnp.bfloat16)
        extra = jnp.concatenate([mine, gains_high, gains_low], axis=1)
        duct_pairs = []
        peers = lax.axis_size(DUCT)
        for i in range(peers):
            target = i - 2 if i % 2 == 0 else i + 2
            if 0 <= target < peers:
                duct_pairs.append((i, target))

    def projection_of(mix, faces, coarse):
        return (
            jnp.dot(mix[:, : faces.shape[0]], faces, preferred_element_type=jnp.float32)
            - jnp.dot(mix[:, faces.shape[0] :], coarse, preferred_element_type=jnp.float32)
        ).astype(jnp.bfloat16)

    def face_rows_of(gain, lower, upper):
        return jnp.concatenate(
            [gain[0][:, None] * lower, gain[1][:, None] * upper], axis=0
        ).astype(jnp.bfloat16)

    base_solve = jnp.dot(inverse, source, preferred_element_type=jnp.float32)
    local_solve = base_solve
    projected = coarse_input(local_solve.astype(jnp.bfloat16))
    if pairwise:
        width = projected.shape[1]
        got = swapped(jnp.concatenate([projected, extra], axis=1), "tile")
        first = tile_index == 0
        inputs = jnp.concatenate(
            [
                jnp.where(first, projected, got[:, :width]),
                jnp.where(first, got[:, :width], projected),
            ],
            axis=0,
        )
        theirs = got[:, width : width + mine.shape[1]]
        tail = got[:, width + mine.shape[1] :].astype(jnp.float32)
        pair = gains.shape[0]
        partner_gains = (tail[:, :pair] + tail[:, pair:]).T
    else:
        inputs = gathered(projected, "tile", 0)
    earlier = None
    for cycle_index in range(ROUNDS):
        coarse = coarse_of(inputs)
        correction = jnp.dot(masked_basis, coarse, preferred_element_type=jnp.float32)
        iterate = local_solve + correction
        if cycle_index == ROUNDS - 1:
            break
        lower_trace = (
            local_solve[lower_at] + jnp.dot(lower_basis, coarse, preferred_element_type=jnp.float32)
        ).astype(jnp.bfloat16)
        upper_trace = (
            local_solve[upper_at] + jnp.dot(upper_basis, coarse, preferred_element_type=jnp.float32)
        ).astype(jnp.bfloat16)
        rows = lower_trace.shape[0]
        if pairwise:
            got_lower = passed_along(jnp.concatenate([upper_trace, coarse], axis=0), 1)
            got_upper = passed_along(jnp.concatenate([lower_trace, coarse], axis=0), -1)
            crossing = lax.ppermute(
                jnp.where(tile_index == 0, lower_trace, upper_trace), DUCT, duct_pairs
            )
            from_lower = got_lower[:rows].astype(jnp.float32)
            from_upper = got_upper[:rows].astype(jnp.float32)
            faces = face_rows_of(gains, from_lower, from_upper)
            first = tile_index == 0
            partner_lower = jnp.where(first, upper_trace, crossing).astype(jnp.float32)
            partner_upper = jnp.where(first, crossing, lower_trace).astype(jnp.float32)
            partner_coarse = jnp.where(first, got_upper[rows:], got_lower[rows:])
            partner_faces = face_rows_of(partner_gains, partner_lower, partner_upper)
            own = projection_of(mine, faces, coarse)
            other = projection_of(theirs, partner_faces, partner_coarse)
            inputs = jnp.concatenate(
                [jnp.where(first, own, other), jnp.where(first, other, own)], axis=0
            )
        else:
            from_lower = passed_along(upper_trace, 1).astype(jnp.float32)
            from_upper = passed_along(lower_trace, -1).astype(jnp.float32)
            faces = face_rows_of(gains, from_lower, from_upper)
        change = jnp.dot(face_inverse, faces, preferred_element_type=jnp.float32)
        local_solve = base_solve + change
        if not pairwise:
            step = change if earlier is None else change - earlier
            inputs = gathered(coarse_input((step - correction).astype(jnp.bfloat16)), "tile", 0)
        earlier = change
    return iterate.astype(jnp.bfloat16)[None]


def solution(mesh):
    placed = (
        P(("group", "sub", "tile"), None, "rep"),
        P(("group", "sub", "tile"), None, None),
        P(("group", "sub", "tile"), None, None),
        P(("group", "sub", "tile"), None, None),
        P(("group", "sub", "tile"), None, None),
        P(("group", "sub", "tile")),
        P("group", "tile", "rep", "sub", None),
    )
    return jax.shard_map(
        local,
        mesh=mesh,
        in_specs=placed,
        out_specs=P(("group", "sub", "tile"), None, "rep"),
        check_vma=False,
    )
```

```python
import jax
import jax.numpy as jnp
from jax import lax
from jax.sharding import PartitionSpec as P

ROUNDS = 2
DUCT = ("sub", "tile")


def passed_along(shard, by):
    peers = lax.axis_size(DUCT)
    pairs = [(i, i + by) for i in range(peers) if 0 <= i + by < peers]
    return lax.ppermute(shard, DUCT, pairs)


def swapped(shard, axis):
    return lax.ppermute(shard, axis, [(0, 1), (1, 0)])


def gathered(shard, axis, dim):
    if lax.axis_size(axis) != 2:
        return lax.all_gather(shard, axis, axis=dim, tiled=True)
    other = swapped(shard, axis)
    first = lax.axis_index(axis) == 0
    return jnp.concatenate(
        [jnp.where(first, shard, other), jnp.where(first, other, shard)], axis=dim
    )


def local(
    right_side,
    interface_inverse,
    coupling,
    trace_rows,
    deflation_basis,
    deflation_counts,
    coarse_inverse,
):
    source = right_side[0]
    inverse = interface_inverse[0]
    iface_rows = inverse.shape[0]
    face_rows = coupling.shape[2]
    slot_count = deflation_basis.shape[2]
    sub_count = lax.axis_size("sub")
    sub_index = lax.axis_index("sub")
    slot_ids = jnp.arange(slot_count, dtype=jnp.int32)
    masked_basis = jnp.where(
        slot_ids[None, :] < deflation_counts[0],
        deflation_basis[0],
        jnp.zeros((), deflation_basis.dtype),
    )
    half_block = coarse_inverse[:, 0, :, 0, :]
    columns = gathered(half_block, "rep", 1)
    lower_gain = coupling[0, 0][:, None]
    upper_gain = coupling[0, 1][:, None]

    lower_at = trace_rows[0, 0]
    upper_at = trace_rows[0, 1]
    lower_basis = masked_basis[lower_at]
    upper_basis = masked_basis[upper_at]
    face_inverse = jnp.concatenate(
        [inverse[:, :face_rows], inverse[:, iface_rows - face_rows :]], axis=1
    )

    def coarse_input(defect):
        return lax.dot_general(
            masked_basis, defect, (((0,), (0,)), ((), ())), preferred_element_type=jnp.float32
        ).astype(jnp.bfloat16)

    def coarse_of(inputs):
        partial = jnp.einsum(
            "jsc,cm->jsm", columns, inputs, preferred_element_type=jnp.float32
        ).astype(jnp.bfloat16)
        total = lax.dynamic_index_in_dim(partial, sub_index, 0, keepdims=False).astype(
            jnp.float32
        )
        for k in range(1, sub_count):
            piece = lax.dynamic_index_in_dim(partial, (sub_index + k) % sub_count, 0, keepdims=False)
            total = total + lax.ppermute(
                piece, "sub", [(i, (i + k) % sub_count) for i in range(sub_count)]
            ).astype(jnp.float32)
        return total.astype(jnp.bfloat16)

    pairwise = lax.axis_size("tile") == 2 and ROUNDS == 2
    tile_index = lax.axis_index("tile")
    gains = coupling[0]
    if pairwise:
        sends = jnp.dot(masked_basis.T, face_inverse, preferred_element_type=jnp.float32)
        keeps = jnp.dot(masked_basis.T, masked_basis, preferred_element_type=jnp.float32)
        mine = jnp.concatenate([sends, keeps], axis=1).astype(jnp.bfloat16)
        gains_high = gains.T.astype(jnp.bfloat16)
        gains_low = (gains.T - gains_high.astype(jnp.float32)).astype(jnp.bfloat16)
        message = jnp.concatenate([mine, gains_high, gains_low], axis=1)
        message, source = lax.optimization_barrier((message, source))
        got = swapped(message, "tile")
        theirs = got[:, : mine.shape[1]]
        tail = got[:, mine.shape[1] :].astype(jnp.float32)
        pair = gains.shape[0]
        partner_gains = (tail[:, :pair] + tail[:, pair:]).T
        duct_pairs = []
        peers = lax.axis_size(DUCT)
        for i in range(peers):
            target = i - 2 if i % 2 == 0 else i + 2
            if 0 <= target < peers:
                duct_pairs.append((i, target))

    def projection_of(mix, faces, coarse):
        return (
            jnp.dot(mix[:, : faces.shape[0]], faces, preferred_element_type=jnp.float32)
            - jnp.dot(mix[:, faces.shape[0] :], coarse, preferred_element_type=jnp.float32)
        ).astype(jnp.bfloat16)

    def face_rows_of(gain, lower, upper):
        return jnp.concatenate(
            [gain[0][:, None] * lower, gain[1][:, None] * upper], axis=0
        ).astype(jnp.bfloat16)

    base_solve = jnp.dot(inverse, source, preferred_element_type=jnp.float32)
    local_solve = base_solve
    inputs = gathered(coarse_input(local_solve.astype(jnp.bfloat16)), "tile", 0)
    earlier = None
    for cycle_index in range(ROUNDS):
        coarse = coarse_of(inputs)
        correction = jnp.dot(masked_basis, coarse, preferred_element_type=jnp.float32)
        iterate = local_solve + correction
        if cycle_index == ROUNDS - 1:
            break
        lower_trace = (
            local_solve[lower_at] + jnp.dot(lower_basis, coarse, preferred_element_type=jnp.float32)
        ).astype(jnp.bfloat16)
        upper_trace = (
            local_solve[upper_at] + jnp.dot(upper_basis, coarse, preferred_element_type=jnp.float32)
        ).astype(jnp.bfloat16)
        rows = lower_trace.shape[0]
        if pairwise:
            got_lower = passed_along(jnp.concatenate([upper_trace, coarse], axis=0), 1)
            got_upper = passed_along(jnp.concatenate([lower_trace, coarse], axis=0), -1)
            crossing = lax.ppermute(
                jnp.where(tile_index == 0, lower_trace, upper_trace), DUCT, duct_pairs
            )
            from_lower = got_lower[:rows].astype(jnp.float32)
            from_upper = got_upper[:rows].astype(jnp.float32)
            faces = face_rows_of(gains, from_lower, from_upper)
            first = tile_index == 0
            partner_lower = jnp.where(first, upper_trace, crossing).astype(jnp.float32)
            partner_upper = jnp.where(first, crossing, lower_trace).astype(jnp.float32)
            partner_coarse = jnp.where(first, got_upper[rows:], got_lower[rows:])
            partner_faces = face_rows_of(partner_gains, partner_lower, partner_upper)
            own = projection_of(mine, faces, coarse)
            other = projection_of(theirs, partner_faces, partner_coarse)
            inputs = jnp.concatenate(
                [jnp.where(first, own, other), jnp.where(first, other, own)], axis=0
            )
        else:
            from_lower = passed_along(upper_trace, 1).astype(jnp.float32)
            from_upper = passed_along(lower_trace, -1).astype(jnp.float32)
            faces = face_rows_of(gains, from_lower, from_upper)
        change = jnp.dot(face_inverse, faces, preferred_element_type=jnp.float32)
        local_solve = base_solve + change
        if not pairwise:
            step = change if earlier is None else change - earlier
            inputs = gathered(coarse_input((step - correction).astype(jnp.bfloat16)), "tile", 0)
        earlier = change
    return iterate.astype(jnp.bfloat16)[None]


def solution(mesh):
    placed = (
        P(("group", "sub", "tile"), None, "rep"),
        P(("group", "sub", "tile"), None, None),
        P(("group", "sub", "tile"), None, None),
        P(("group", "sub", "tile"), None, None),
        P(("group", "sub", "tile"), None, None),
        P(("group", "sub", "tile")),
        P("group", "tile", "rep", "sub", None),
    )
    return jax.shard_map(
        local,
        mesh=mesh,
        in_specs=placed,
        out_specs=P(("group", "sub", "tile"), None, "rep"),
        check_vma=False,
    )
```

```python
import jax
import jax.numpy as jnp
from jax import lax
from jax.sharding import PartitionSpec as P

ROUNDS = 2
DUCT = ("sub", "tile")


def passed_along(shard, by):
    peers = lax.axis_size(DUCT)
    pairs = [(i, i + by) for i in range(peers) if 0 <= i + by < peers]
    return lax.ppermute(shard, DUCT, pairs)


def swapped(shard, axis):
    return lax.ppermute(shard, axis, [(0, 1), (1, 0)])


def gathered(shard, axis, dim):
    if lax.axis_size(axis) != 2:
        return lax.all_gather(shard, axis, axis=dim, tiled=True)
    other = swapped(shard, axis)
    first = lax.axis_index(axis) == 0
    return jnp.concatenate(
        [jnp.where(first, shard, other), jnp.where(first, other, shard)], axis=dim
    )


def local(
    right_side,
    interface_inverse,
    coupling,
    trace_rows,
    deflation_basis,
    deflation_counts,
    coarse_inverse,
):
    source = right_side[0]
    inverse = interface_inverse[0]
    iface_rows = inverse.shape[0]
    face_rows = coupling.shape[2]
    slot_count = deflation_basis.shape[2]
    sub_count = lax.axis_size("sub")
    sub_index = lax.axis_index("sub")
    slot_ids = jnp.arange(slot_count, dtype=jnp.int32)
    masked_basis = jnp.where(
        slot_ids[None, :] < deflation_counts[0],
        deflation_basis[0],
        jnp.zeros((), deflation_basis.dtype),
    )
    half_block = coarse_inverse[:, 0, :, 0, :]
    columns = gathered(half_block, "rep", 1)
    lower_gain = coupling[0, 0][:, None]
    upper_gain = coupling[0, 1][:, None]

    lower_at = trace_rows[0, 0]
    upper_at = trace_rows[0, 1]
    lower_basis = masked_basis[lower_at]
    upper_basis = masked_basis[upper_at]
    face_inverse = jnp.concatenate(
        [inverse[:, :face_rows], inverse[:, iface_rows - face_rows :]], axis=1
    )

    def coarse_input(defect):
        return lax.dot_general(
            masked_basis, defect, (((0,), (0,)), ((), ())), preferred_element_type=jnp.float32
        ).astype(jnp.bfloat16)

    def coarse_of(inputs):
        partial = jnp.einsum(
            "jsc,cm->jsm", columns, inputs, preferred_element_type=jnp.float32
        ).astype(jnp.bfloat16)
        total = lax.dynamic_index_in_dim(partial, sub_index, 0, keepdims=False).astype(
            jnp.float32
        )
        for k in range(1, sub_count):
            piece = lax.dynamic_index_in_dim(partial, (sub_index + k) % sub_count, 0, keepdims=False)
            total = total + lax.ppermute(
                piece, "sub", [(i, (i + k) % sub_count) for i in range(sub_count)]
            ).astype(jnp.float32)
        return total.astype(jnp.bfloat16)

    pairwise = lax.axis_size("tile") == 2 and ROUNDS == 2
    tile_index = lax.axis_index("tile")
    gains = coupling[0]
    if pairwise:
        sends = jnp.dot(masked_basis.T, face_inverse, preferred_element_type=jnp.float32)
        keeps = jnp.dot(masked_basis.T, masked_basis, preferred_element_type=jnp.float32)
        mine = jnp.concatenate([sends, keeps], axis=1).astype(jnp.bfloat16)
        gains_high = gains.T.astype(jnp.bfloat16)
        gains_low = (gains.T - gains_high.astype(jnp.float32)).astype(jnp.bfloat16)
        gains_pair = jnp.concatenate([gains_high, gains_low], axis=1)
        peers = lax.axis_size(DUCT)
        diagonal_pairs = []
        crossing_pairs = []
        for i in range(peers):
            target = i - 1 if i % 2 == 0 else i + 1
            if 0 <= target < peers:
                diagonal_pairs.append((i, target))
            target = i - 2 if i % 2 == 0 else i + 2
            if 0 <= target < peers:
                crossing_pairs.append((i, target))

    def projection_of(mix, faces, coarse):
        return (
            jnp.dot(mix[:, : faces.shape[0]], faces, preferred_element_type=jnp.float32)
            - jnp.dot(mix[:, faces.shape[0] :], coarse, preferred_element_type=jnp.float32)
        ).astype(jnp.bfloat16)

    def face_rows_of(gain, lower, upper):
        return jnp.concatenate(
            [gain[0][:, None] * lower, gain[1][:, None] * upper], axis=0
        ).astype(jnp.bfloat16)

    base_solve = jnp.dot(inverse, source, preferred_element_type=jnp.float32)
    local_solve = base_solve
    projected = coarse_input(local_solve.astype(jnp.bfloat16))
    if pairwise:
        width = projected.shape[1]
        got = swapped(jnp.concatenate([projected, gains_pair], axis=1), "tile")
        first = tile_index == 0
        inputs = jnp.concatenate(
            [
                jnp.where(first, projected, got[:, :width]),
                jnp.where(first, got[:, :width], projected),
            ],
            axis=0,
        )
        tail = got[:, width:].astype(jnp.float32)
        pair = gains.shape[0]
        partner_gains = (tail[:, :pair] + tail[:, pair:]).T
    else:
        inputs = gathered(projected, "tile", 0)
    earlier = None
    for cycle_index in range(ROUNDS):
        coarse = coarse_of(inputs)
        correction = jnp.dot(masked_basis, coarse, preferred_element_type=jnp.float32)
        iterate = local_solve + correction
        if cycle_index == ROUNDS - 1:
            break
        lower_trace = (
            local_solve[lower_at] + jnp.dot(lower_basis, coarse, preferred_element_type=jnp.float32)
        ).astype(jnp.bfloat16)
        upper_trace = (
            local_solve[upper_at] + jnp.dot(upper_basis, coarse, preferred_element_type=jnp.float32)
        ).astype(jnp.bfloat16)
        rows = lower_trace.shape[0]
        if pairwise:
            toward_partner = jnp.where(first, upper_trace, lower_trace)
            toward_diagonal = jnp.where(first, lower_trace, upper_trace)
            width = toward_partner.shape[1]
            got = swapped(jnp.concatenate([toward_partner, coarse, mine], axis=1), "tile")
            from_diagonal = lax.ppermute(toward_diagonal, DUCT, diagonal_pairs)
            crossing = lax.ppermute(toward_diagonal, DUCT, crossing_pairs)
            from_partner = got[:, :width]
            from_lower = jnp.where(first, from_diagonal, from_partner).astype(jnp.float32)
            from_upper = jnp.where(first, from_partner, from_diagonal).astype(jnp.float32)
            faces = face_rows_of(gains, from_lower, from_upper)
            partner_lower = jnp.where(first, upper_trace, crossing).astype(jnp.float32)
            partner_upper = jnp.where(first, crossing, lower_trace).astype(jnp.float32)
            partner_coarse = got[:, width : 2 * width]
            theirs = got[:, 2 * width :]
            partner_faces = face_rows_of(partner_gains, partner_lower, partner_upper)
            own = projection_of(mine, faces, coarse)
            other = projection_of(theirs, partner_faces, partner_coarse)
            inputs = jnp.concatenate(
                [jnp.where(first, own, other), jnp.where(first, other, own)], axis=0
            )
        else:
            from_lower = passed_along(upper_trace, 1).astype(jnp.float32)
            from_upper = passed_along(lower_trace, -1).astype(jnp.float32)
            faces = face_rows_of(gains, from_lower, from_upper)
        change = jnp.dot(face_inverse, faces, preferred_element_type=jnp.float32)
        local_solve = base_solve + change
        if not pairwise:
            step = change if earlier is None else change - earlier
            inputs = gathered(coarse_input((step - correction).astype(jnp.bfloat16)), "tile", 0)
        earlier = change
    return iterate.astype(jnp.bfloat16)[None]


def solution(mesh):
    placed = (
        P(("group", "sub", "tile"), None, "rep"),
        P(("group", "sub", "tile"), None, None),
        P(("group", "sub", "tile"), None, None),
        P(("group", "sub", "tile"), None, None),
        P(("group", "sub", "tile"), None, None),
        P(("group", "sub", "tile")),
        P("group", "tile", "rep", "sub", None),
    )
    return jax.shard_map(
        local,
        mesh=mesh,
        in_specs=placed,
        out_specs=P(("group", "sub", "tile"), None, "rep"),
        check_vma=False,
    )
```

```python
import jax
import jax.numpy as jnp
from jax import lax
from jax.sharding import PartitionSpec as P

ROUNDS = 2
DUCT = ("sub", "tile")


def passed_along(shard, by):
    peers = lax.axis_size(DUCT)
    pairs = [(i, i + by) for i in range(peers) if 0 <= i + by < peers]
    return lax.ppermute(shard, DUCT, pairs)


def swapped(shard, axis):
    return lax.ppermute(shard, axis, [(0, 1), (1, 0)])


def gathered(shard, axis, dim):
    if lax.axis_size(axis) != 2:
        return lax.all_gather(shard, axis, axis=dim, tiled=True)
    other = swapped(shard, axis)
    first = lax.axis_index(axis) == 0
    return jnp.concatenate(
        [jnp.where(first, shard, other), jnp.where(first, other, shard)], axis=dim
    )


def local(
    right_side,
    interface_inverse,
    coupling,
    trace_rows,
    deflation_basis,
    deflation_counts,
    coarse_inverse,
):
    source = right_side[0]
    inverse = interface_inverse[0]
    iface_rows = inverse.shape[0]
    face_rows = coupling.shape[2]
    slot_count = deflation_basis.shape[2]
    sub_count = lax.axis_size("sub")
    sub_index = lax.axis_index("sub")
    slot_ids = jnp.arange(slot_count, dtype=jnp.int32)
    masked_basis = jnp.where(
        slot_ids[None, :] < deflation_counts[0],
        deflation_basis[0],
        jnp.zeros((), deflation_basis.dtype),
    )
    half_block = coarse_inverse[:, 0, :, 0, :]
    columns = gathered(half_block, "rep", 1)
    lower_gain = coupling[0, 0][:, None]
    upper_gain = coupling[0, 1][:, None]

    lower_at = trace_rows[0, 0]
    upper_at = trace_rows[0, 1]
    lower_basis = masked_basis[lower_at]
    upper_basis = masked_basis[upper_at]
    face_inverse = jnp.concatenate(
        [inverse[:, :face_rows], inverse[:, iface_rows - face_rows :]], axis=1
    )

    def coarse_input(defect):
        return lax.dot_general(
            masked_basis, defect, (((0,), (0,)), ((), ())), preferred_element_type=jnp.float32
        ).astype(jnp.bfloat16)

    def coarse_of(inputs):
        partial = jnp.einsum(
            "jsc,cm->jsm", columns, inputs, preferred_element_type=jnp.float32
        ).astype(jnp.bfloat16)
        total = lax.dynamic_index_in_dim(partial, sub_index, 0, keepdims=False).astype(
            jnp.float32
        )
        for k in range(1, sub_count):
            piece = lax.dynamic_index_in_dim(partial, (sub_index + k) % sub_count, 0, keepdims=False)
            total = total + lax.ppermute(
                piece, "sub", [(i, (i + k) % sub_count) for i in range(sub_count)]
            ).astype(jnp.float32)
        return total.astype(jnp.bfloat16)

    pairwise = lax.axis_size("tile") == 2 and ROUNDS == 2
    tile_index = lax.axis_index("tile")
    gains = coupling[0]
    if pairwise:
        sends = jnp.dot(masked_basis.T, face_inverse, preferred_element_type=jnp.float32)
        keeps = jnp.dot(masked_basis.T, masked_basis, preferred_element_type=jnp.float32)
        mine = jnp.concatenate([sends, keeps], axis=1).astype(jnp.bfloat16)
        gains_high = gains.T.astype(jnp.bfloat16)
        gains_low = (gains.T - gains_high.astype(jnp.float32)).astype(jnp.bfloat16)
        message = jnp.concatenate([mine, gains_high, gains_low], axis=1)
        duct_pairs = []
        peers = lax.axis_size(DUCT)
        for i in range(peers):
            target = i - 2 if i % 2 == 0 else i + 2
            if 0 <= target < peers:
                duct_pairs.append((i, target))

    def projection_of(mix, faces, coarse):
        return (
            jnp.dot(mix[:, : faces.shape[0]], faces, preferred_element_type=jnp.float32)
            - jnp.dot(mix[:, faces.shape[0] :], coarse, preferred_element_type=jnp.float32)
        ).astype(jnp.bfloat16)

    def face_rows_of(gain, lower, upper):
        return jnp.concatenate(
            [gain[0][:, None] * lower, gain[1][:, None] * upper], axis=0
        ).astype(jnp.bfloat16)

    base_solve = jnp.dot(inverse, source, preferred_element_type=jnp.float32)
    local_solve = base_solve
    inputs = gathered(coarse_input(local_solve.astype(jnp.bfloat16)), "tile", 0)
    if pairwise:
        message, inputs = lax.optimization_barrier((message, inputs))
        got = swapped(message, "tile")
        theirs = got[:, : mine.shape[1]]
        tail = got[:, mine.shape[1] :].astype(jnp.float32)
        pair = gains.shape[0]
        partner_gains = (tail[:, :pair] + tail[:, pair:]).T
    earlier = None
    for cycle_index in range(ROUNDS):
        coarse = coarse_of(inputs)
        correction = jnp.dot(masked_basis, coarse, preferred_element_type=jnp.float32)
        iterate = local_solve + correction
        if cycle_index == ROUNDS - 1:
            break
        lower_trace = (
            local_solve[lower_at] + jnp.dot(lower_basis, coarse, preferred_element_type=jnp.float32)
        ).astype(jnp.bfloat16)
        upper_trace = (
            local_solve[upper_at] + jnp.dot(upper_basis, coarse, preferred_element_type=jnp.float32)
        ).astype(jnp.bfloat16)
        rows = lower_trace.shape[0]
        if pairwise:
            got_lower = passed_along(jnp.concatenate([upper_trace, coarse], axis=0), 1)
            got_upper = passed_along(jnp.concatenate([lower_trace, coarse], axis=0), -1)
            crossing = lax.ppermute(
                jnp.where(tile_index == 0, lower_trace, upper_trace), DUCT, duct_pairs
            )
            from_lower = got_lower[:rows].astype(jnp.float32)
            from_upper = got_upper[:rows].astype(jnp.float32)
            faces = face_rows_of(gains, from_lower, from_upper)
            first = tile_index == 0
            partner_lower = jnp.where(first, upper_trace, crossing).astype(jnp.float32)
            partner_upper = jnp.where(first, crossing, lower_trace).astype(jnp.float32)
            partner_coarse = jnp.where(first, got_upper[rows:], got_lower[rows:])
            partner_faces = face_rows_of(partner_gains, partner_lower, partner_upper)
            own = projection_of(mine, faces, coarse)
            other = projection_of(theirs, partner_faces, partner_coarse)
            inputs = jnp.concatenate(
                [jnp.where(first, own, other), jnp.where(first, other, own)], axis=0
            )
        else:
            from_lower = passed_along(upper_trace, 1).astype(jnp.float32)
            from_upper = passed_along(lower_trace, -1).astype(jnp.float32)
            faces = face_rows_of(gains, from_lower, from_upper)
        change = jnp.dot(face_inverse, faces, preferred_element_type=jnp.float32)
        local_solve = base_solve + change
        if not pairwise:
            step = change if earlier is None else change - earlier
            inputs = gathered(coarse_input((step - correction).astype(jnp.bfloat16)), "tile", 0)
        earlier = change
    return iterate.astype(jnp.bfloat16)[None]


def solution(mesh):
    placed = (
        P(("group", "sub", "tile"), None, "rep"),
        P(("group", "sub", "tile"), None, None),
        P(("group", "sub", "tile"), None, None),
        P(("group", "sub", "tile"), None, None),
        P(("group", "sub", "tile"), None, None),
        P(("group", "sub", "tile")),
        P("group", "tile", "rep", "sub", None),
    )
    return jax.shard_map(
        local,
        mesh=mesh,
        in_specs=placed,
        out_specs=P(("group", "sub", "tile"), None, "rep"),
        check_vma=False,
    )
```

```python
import jax
import jax.numpy as jnp
from jax import lax
from jax.sharding import PartitionSpec as P

ROUNDS = 2
DUCT = ("sub", "tile")


def passed_along(shard, by):
    peers = lax.axis_size(DUCT)
    pairs = [(i, i + by) for i in range(peers) if 0 <= i + by < peers]
    return lax.ppermute(shard, DUCT, pairs)


def swapped(shard, axis):
    return lax.ppermute(shard, axis, [(0, 1), (1, 0)])


def gathered(shard, axis, dim):
    if lax.axis_size(axis) != 2:
        return lax.all_gather(shard, axis, axis=dim, tiled=True)
    other = swapped(shard, axis)
    first = lax.axis_index(axis) == 0
    return jnp.concatenate(
        [jnp.where(first, shard, other), jnp.where(first, other, shard)], axis=dim
    )


def local(
    right_side,
    interface_inverse,
    coupling,
    trace_rows,
    deflation_basis,
    deflation_counts,
    coarse_inverse,
):
    source = right_side[0]
    inverse = interface_inverse[0]
    iface_rows = inverse.shape[0]
    face_rows = coupling.shape[2]
    slot_count = deflation_basis.shape[2]
    sub_count = lax.axis_size("sub")
    sub_index = lax.axis_index("sub")
    slot_ids = jnp.arange(slot_count, dtype=jnp.int32)
    masked_basis = jnp.where(
        slot_ids[None, :] < deflation_counts[0],
        deflation_basis[0],
        jnp.zeros((), deflation_basis.dtype),
    )
    half_block = coarse_inverse[:, 0, :, 0, :]
    columns = gathered(half_block, "rep", 1)
    lower_gain = coupling[0, 0][:, None]
    upper_gain = coupling[0, 1][:, None]

    lower_at = trace_rows[0, 0]
    upper_at = trace_rows[0, 1]
    trace_at = jnp.concatenate([lower_at, upper_at])
    trace_basis = jnp.take(masked_basis, trace_at, axis=0)
    lower_basis = trace_basis[: lower_at.shape[0]]
    upper_basis = trace_basis[lower_at.shape[0] :]
    trace_solve = jnp.dot(
        jnp.take(inverse, trace_at, axis=0), source, preferred_element_type=jnp.float32
    )
    face_inverse = jnp.concatenate(
        [inverse[:, :face_rows], inverse[:, iface_rows - face_rows :]], axis=1
    )

    def coarse_input(defect):
        return lax.dot_general(
            masked_basis, defect, (((0,), (0,)), ((), ())), preferred_element_type=jnp.float32
        ).astype(jnp.bfloat16)

    def coarse_of(inputs):
        partial = jnp.einsum(
            "jsc,cm->jsm", columns, inputs, preferred_element_type=jnp.float32
        ).astype(jnp.bfloat16)
        total = lax.dynamic_index_in_dim(partial, sub_index, 0, keepdims=False).astype(
            jnp.float32
        )
        for k in range(1, sub_count):
            piece = lax.dynamic_index_in_dim(partial, (sub_index + k) % sub_count, 0, keepdims=False)
            total = total + lax.ppermute(
                piece, "sub", [(i, (i + k) % sub_count) for i in range(sub_count)]
            ).astype(jnp.float32)
        return total.astype(jnp.bfloat16)

    pairwise = lax.axis_size("tile") == 2 and ROUNDS == 2
    tile_index = lax.axis_index("tile")
    gains = coupling[0]
    if pairwise:
        sends = jnp.dot(masked_basis.T, face_inverse, preferred_element_type=jnp.float32)
        keeps = jnp.dot(masked_basis.T, masked_basis, preferred_element_type=jnp.float32)
        mine = jnp.concatenate([sends, keeps], axis=1).astype(jnp.bfloat16)
        gains_high = gains.T.astype(jnp.bfloat16)
        gains_low = (gains.T - gains_high.astype(jnp.float32)).astype(jnp.bfloat16)
        message = jnp.concatenate([mine, gains_high, gains_low], axis=1)
        duct_pairs = []
        peers = lax.axis_size(DUCT)
        for i in range(peers):
            target = i - 2 if i % 2 == 0 else i + 2
            if 0 <= target < peers:
                duct_pairs.append((i, target))

    def projection_of(mix, faces, coarse):
        return (
            jnp.dot(mix[:, : faces.shape[0]], faces, preferred_element_type=jnp.float32)
            - jnp.dot(mix[:, faces.shape[0] :], coarse, preferred_element_type=jnp.float32)
        ).astype(jnp.bfloat16)

    def face_rows_of(gain, lower, upper):
        return jnp.concatenate(
            [gain[0][:, None] * lower, gain[1][:, None] * upper], axis=0
        ).astype(jnp.bfloat16)

    base_solve = jnp.dot(inverse, source, preferred_element_type=jnp.float32)
    local_solve = base_solve
    inputs = gathered(coarse_input(local_solve.astype(jnp.bfloat16)), "tile", 0)
    if pairwise:
        message, inputs = lax.optimization_barrier((message, inputs))
        got = swapped(message, "tile")
        theirs = got[:, : mine.shape[1]]
        tail = got[:, mine.shape[1] :].astype(jnp.float32)
        pair = gains.shape[0]
        partner_gains = (tail[:, :pair] + tail[:, pair:]).T
    earlier = None
    for cycle_index in range(ROUNDS):
        coarse = coarse_of(inputs)
        correction = jnp.dot(masked_basis, coarse, preferred_element_type=jnp.float32)
        iterate = local_solve + correction
        if cycle_index == ROUNDS - 1:
            break
        if cycle_index == 0:
            solve_rows = trace_solve
        else:
            solve_rows = jnp.take(local_solve, trace_at, axis=0)
        traces = (
            solve_rows + jnp.dot(trace_basis, coarse, preferred_element_type=jnp.float32)
        ).astype(jnp.bfloat16)
        rows = lower_at.shape[0]
        lower_trace = traces[:rows]
        upper_trace = traces[rows:]
        if pairwise:
            got_lower = passed_along(jnp.concatenate([upper_trace, coarse], axis=0), 1)
            got_upper = passed_along(jnp.concatenate([lower_trace, coarse], axis=0), -1)
            crossing = lax.ppermute(
                jnp.where(tile_index == 0, lower_trace, upper_trace), DUCT, duct_pairs
            )
            from_lower = got_lower[:rows].astype(jnp.float32)
            from_upper = got_upper[:rows].astype(jnp.float32)
            faces = face_rows_of(gains, from_lower, from_upper)
            first = tile_index == 0
            partner_lower = jnp.where(first, upper_trace, crossing).astype(jnp.float32)
            partner_upper = jnp.where(first, crossing, lower_trace).astype(jnp.float32)
            partner_coarse = jnp.where(first, got_upper[rows:], got_lower[rows:])
            partner_faces = face_rows_of(partner_gains, partner_lower, partner_upper)
            own = projection_of(mine, faces, coarse)
            other = projection_of(theirs, partner_faces, partner_coarse)
            inputs = jnp.concatenate(
                [jnp.where(first, own, other), jnp.where(first, other, own)], axis=0
            )
        else:
            from_lower = passed_along(upper_trace, 1).astype(jnp.float32)
            from_upper = passed_along(lower_trace, -1).astype(jnp.float32)
            faces = face_rows_of(gains, from_lower, from_upper)
        change = jnp.dot(face_inverse, faces, preferred_element_type=jnp.float32)
        local_solve = base_solve + change
        if not pairwise:
            step = change if earlier is None else change - earlier
            inputs = gathered(coarse_input((step - correction).astype(jnp.bfloat16)), "tile", 0)
        earlier = change
    return iterate.astype(jnp.bfloat16)[None]


def solution(mesh):
    placed = (
        P(("group", "sub", "tile"), None, "rep"),
        P(("group", "sub", "tile"), None, None),
        P(("group", "sub", "tile"), None, None),
        P(("group", "sub", "tile"), None, None),
        P(("group", "sub", "tile"), None, None),
        P(("group", "sub", "tile")),
        P("group", "tile", "rep", "sub", None),
    )
    return jax.shard_map(
        local,
        mesh=mesh,
        in_specs=placed,
        out_specs=P(("group", "sub", "tile"), None, "rep"),
        check_vma=False,
    )
```

```python
import jax
import jax.numpy as jnp
from jax import lax
from jax.sharding import PartitionSpec as P

ROUNDS = 2
DUCT = ("sub", "tile")


def passed_along(shard, by):
    peers = lax.axis_size(DUCT)
    pairs = [(i, i + by) for i in range(peers) if 0 <= i + by < peers]
    return lax.ppermute(shard, DUCT, pairs)


def swapped(shard, axis):
    return lax.ppermute(shard, axis, [(0, 1), (1, 0)])


def gathered(shard, axis, dim):
    if lax.axis_size(axis) != 2:
        return lax.all_gather(shard, axis, axis=dim, tiled=True)
    other = swapped(shard, axis)
    first = lax.axis_index(axis) == 0
    return jnp.concatenate(
        [jnp.where(first, shard, other), jnp.where(first, other, shard)], axis=dim
    )


def local(
    right_side,
    interface_inverse,
    coupling,
    trace_rows,
    deflation_basis,
    deflation_counts,
    coarse_inverse,
):
    source = right_side[0]
    inverse = interface_inverse[0]
    iface_rows = inverse.shape[0]
    face_rows = coupling.shape[2]
    slot_count = deflation_basis.shape[2]
    sub_count = lax.axis_size("sub")
    sub_index = lax.axis_index("sub")
    slot_ids = jnp.arange(slot_count, dtype=jnp.int32)
    basis = deflation_basis[0]
    live = (slot_ids < deflation_counts[0])[:, None]
    half_block = coarse_inverse[:, 0, :, 0, :]
    columns = gathered(half_block, "rep", 1)
    lower_gain = coupling[0, 0][:, None]
    upper_gain = coupling[0, 1][:, None]

    lower_at = trace_rows[0, 0]
    upper_at = trace_rows[0, 1]
    lower_basis = basis[lower_at]
    upper_basis = basis[upper_at]
    face_inverse = jnp.concatenate(
        [inverse[:, :face_rows], inverse[:, iface_rows - face_rows :]], axis=1
    )

    def coarse_input(defect):
        projected = lax.dot_general(
            basis, defect, (((0,), (0,)), ((), ())), preferred_element_type=jnp.float32
        )
        return jnp.where(live, projected, 0.0).astype(jnp.bfloat16)

    def coarse_of(inputs):
        partial = jnp.einsum(
            "jsc,cm->jsm", columns, inputs, preferred_element_type=jnp.float32
        ).astype(jnp.bfloat16)
        total = lax.dynamic_index_in_dim(partial, sub_index, 0, keepdims=False).astype(
            jnp.float32
        )
        for k in range(1, sub_count):
            piece = lax.dynamic_index_in_dim(partial, (sub_index + k) % sub_count, 0, keepdims=False)
            total = total + lax.ppermute(
                piece, "sub", [(i, (i + k) % sub_count) for i in range(sub_count)]
            ).astype(jnp.float32)
        return total.astype(jnp.bfloat16)

    pairwise = lax.axis_size("tile") == 2 and ROUNDS == 2
    tile_index = lax.axis_index("tile")
    gains = coupling[0]
    if pairwise:
        sends = jnp.where(
            live, jnp.dot(basis.T, face_inverse, preferred_element_type=jnp.float32), 0.0
        )
        keeps = jnp.where(
            live & live.T, jnp.dot(basis.T, basis, preferred_element_type=jnp.float32), 0.0
        )
        mine = jnp.concatenate([sends, keeps], axis=1).astype(jnp.bfloat16)
        gains_high = gains.T.astype(jnp.bfloat16)
        gains_low = (gains.T - gains_high.astype(jnp.float32)).astype(jnp.bfloat16)
        gains_pair = jnp.concatenate([gains_high, gains_low], axis=1)
        peers = lax.axis_size(DUCT)
        diagonal_pairs = []
        crossing_pairs = []
        for i in range(peers):
            target = i - 1 if i % 2 == 0 else i + 1
            if 0 <= target < peers:
                diagonal_pairs.append((i, target))
            target = i - 2 if i % 2 == 0 else i + 2
            if 0 <= target < peers:
                crossing_pairs.append((i, target))

    def projection_of(mix, faces, coarse):
        return (
            jnp.dot(mix[:, : faces.shape[0]], faces, preferred_element_type=jnp.float32)
            - jnp.dot(mix[:, faces.shape[0] :], coarse, preferred_element_type=jnp.float32)
        ).astype(jnp.bfloat16)

    def face_rows_of(gain, lower, upper):
        return jnp.concatenate(
            [gain[0][:, None] * lower, gain[1][:, None] * upper], axis=0
        ).astype(jnp.bfloat16)

    base_solve = jnp.dot(inverse, source, preferred_element_type=jnp.float32)
    local_solve = base_solve
    projected = coarse_input(local_solve.astype(jnp.bfloat16))
    if pairwise:
        width = projected.shape[1]
        got = swapped(jnp.concatenate([projected, gains_pair], axis=1), "tile")
        first = tile_index == 0
        inputs = jnp.concatenate(
            [
                jnp.where(first, projected, got[:, :width]),
                jnp.where(first, got[:, :width], projected),
            ],
            axis=0,
        )
        tail = got[:, width:].astype(jnp.float32)
        pair = gains.shape[0]
        partner_gains = (tail[:, :pair] + tail[:, pair:]).T
    else:
        inputs = gathered(projected, "tile", 0)
    earlier = None
    for cycle_index in range(ROUNDS):
        coarse = coarse_of(inputs)
        coarse = jnp.where(live, coarse, jnp.zeros((), coarse.dtype))
        correction = jnp.dot(basis, coarse, preferred_element_type=jnp.float32)
        iterate = local_solve + correction
        if cycle_index == ROUNDS - 1:
            break
        lower_trace = (
            local_solve[lower_at] + jnp.dot(lower_basis, coarse, preferred_element_type=jnp.float32)
        ).astype(jnp.bfloat16)
        upper_trace = (
            local_solve[upper_at] + jnp.dot(upper_basis, coarse, preferred_element_type=jnp.float32)
        ).astype(jnp.bfloat16)
        rows = lower_trace.shape[0]
        if pairwise:
            toward_partner = jnp.where(first, upper_trace, lower_trace)
            toward_diagonal = jnp.where(first, lower_trace, upper_trace)
            width = toward_partner.shape[1]
            got = swapped(jnp.concatenate([toward_partner, coarse, mine], axis=1), "tile")
            from_diagonal = lax.ppermute(toward_diagonal, DUCT, diagonal_pairs)
            crossing = lax.ppermute(toward_diagonal, DUCT, crossing_pairs)
            from_partner = got[:, :width]
            from_lower = jnp.where(first, from_diagonal, from_partner).astype(jnp.float32)
            from_upper = jnp.where(first, from_partner, from_diagonal).astype(jnp.float32)
            faces = face_rows_of(gains, from_lower, from_upper)
            partner_lower = jnp.where(first, upper_trace, crossing).astype(jnp.float32)
            partner_upper = jnp.where(first, crossing, lower_trace).astype(jnp.float32)
            partner_coarse = got[:, width : 2 * width]
            theirs = got[:, 2 * width :]
            partner_faces = face_rows_of(partner_gains, partner_lower, partner_upper)
            own = projection_of(mine, faces, coarse)
            other = projection_of(theirs, partner_faces, partner_coarse)
            inputs = jnp.concatenate(
                [jnp.where(first, own, other), jnp.where(first, other, own)], axis=0
            )
        else:
            from_lower = passed_along(upper_trace, 1).astype(jnp.float32)
            from_upper = passed_along(lower_trace, -1).astype(jnp.float32)
            faces = face_rows_of(gains, from_lower, from_upper)
        change = jnp.dot(face_inverse, faces, preferred_element_type=jnp.float32)
        local_solve = base_solve + change
        if not pairwise:
            step = change if earlier is None else change - earlier
            inputs = gathered(coarse_input((step - correction).astype(jnp.bfloat16)), "tile", 0)
        earlier = change
    return iterate.astype(jnp.bfloat16)[None]


def solution(mesh):
    placed = (
        P(("group", "sub", "tile"), None, "rep"),
        P(("group", "sub", "tile"), None, None),
        P(("group", "sub", "tile"), None, None),
        P(("group", "sub", "tile"), None, None),
        P(("group", "sub", "tile"), None, None),
        P(("group", "sub", "tile")),
        P("group", "tile", "rep", "sub", None),
    )
    return jax.shard_map(
        local,
        mesh=mesh,
        in_specs=placed,
        out_specs=P(("group", "sub", "tile"), None, "rep"),
        check_vma=False,
    )
```

```python
import jax
import jax.numpy as jnp
from jax import lax
from jax.sharding import PartitionSpec as P

ROUNDS = 2
DUCT = ("sub", "tile")


def passed_along(shard, by):
    peers = lax.axis_size(DUCT)
    pairs = [(i, i + by) for i in range(peers) if 0 <= i + by < peers]
    return lax.ppermute(shard, DUCT, pairs)


def swapped(shard, axis):
    return lax.ppermute(shard, axis, [(0, 1), (1, 0)])


def gathered(shard, axis, dim):
    if lax.axis_size(axis) != 2:
        return lax.all_gather(shard, axis, axis=dim, tiled=True)
    other = swapped(shard, axis)
    first = lax.axis_index(axis) == 0
    return jnp.concatenate(
        [jnp.where(first, shard, other), jnp.where(first, other, shard)], axis=dim
    )


def local(
    right_side,
    interface_inverse,
    coupling,
    trace_rows,
    deflation_basis,
    deflation_counts,
    coarse_inverse,
):
    source = right_side[0]
    inverse = interface_inverse[0]
    iface_rows = inverse.shape[0]
    face_rows = coupling.shape[2]
    slot_count = deflation_basis.shape[2]
    sub_count = lax.axis_size("sub")
    sub_index = lax.axis_index("sub")
    slot_ids = jnp.arange(slot_count, dtype=jnp.int32)
    basis = deflation_basis[0]
    live = (slot_ids < deflation_counts[0])[:, None]
    half_block = coarse_inverse[:, 0, :, 0, :]
    columns = gathered(half_block, "rep", 1)
    lower_gain = coupling[0, 0][:, None]
    upper_gain = coupling[0, 1][:, None]

    lower_at = trace_rows[0, 0]
    upper_at = trace_rows[0, 1]
    face_inverse = jnp.concatenate(
        [inverse[:, :face_rows], inverse[:, iface_rows - face_rows :]], axis=1
    )

    def coarse_input(defect):
        projected = lax.dot_general(
            basis, defect, (((0,), (0,)), ((), ())), preferred_element_type=jnp.float32
        )
        return jnp.where(live, projected, 0.0).astype(jnp.bfloat16)

    def coarse_of(inputs, riders):
        partial = jnp.einsum(
            "jsc,cm->jsm", columns, inputs, preferred_element_type=jnp.float32
        ).astype(jnp.bfloat16)
        partial, riders = lax.optimization_barrier((partial, riders))
        total = lax.dynamic_index_in_dim(partial, sub_index, 0, keepdims=False).astype(
            jnp.float32
        )
        for k in range(1, sub_count):
            piece = lax.dynamic_index_in_dim(partial, (sub_index + k) % sub_count, 0, keepdims=False)
            total = total + lax.ppermute(
                piece, "sub", [(i, (i + k) % sub_count) for i in range(sub_count)]
            ).astype(jnp.float32)
        return total.astype(jnp.bfloat16), riders

    pairwise = lax.axis_size("tile") == 2 and ROUNDS == 2
    tile_index = lax.axis_index("tile")
    gains = coupling[0]
    if pairwise:
        gains_high = gains.T.astype(jnp.bfloat16)
        gains_low = (gains.T - gains_high.astype(jnp.float32)).astype(jnp.bfloat16)
        gains_pair = jnp.concatenate([gains_high, gains_low], axis=1)
        peers = lax.axis_size(DUCT)
        diagonal_pairs = []
        crossing_pairs = []
        for i in range(peers):
            target = i - 1 if i % 2 == 0 else i + 1
            if 0 <= target < peers:
                diagonal_pairs.append((i, target))
            target = i - 2 if i % 2 == 0 else i + 2
            if 0 <= target < peers:
                crossing_pairs.append((i, target))

    def projection_of(mix, faces, coarse):
        return (
            jnp.dot(mix[:, : faces.shape[0]], faces, preferred_element_type=jnp.float32)
            - jnp.dot(mix[:, faces.shape[0] :], coarse, preferred_element_type=jnp.float32)
        ).astype(jnp.bfloat16)

    def face_rows_of(gain, lower, upper):
        return jnp.concatenate(
            [gain[0][:, None] * lower, gain[1][:, None] * upper], axis=0
        ).astype(jnp.bfloat16)

    base_solve = jnp.dot(inverse, source, preferred_element_type=jnp.float32)
    local_solve = base_solve
    projected = coarse_input(local_solve.astype(jnp.bfloat16))
    if pairwise:
        width = projected.shape[1]
        got = swapped(jnp.concatenate([projected, gains_pair], axis=1), "tile")
        first = tile_index == 0
        inputs = jnp.concatenate(
            [
                jnp.where(first, projected, got[:, :width]),
                jnp.where(first, got[:, :width], projected),
            ],
            axis=0,
        )
        tail = got[:, width:].astype(jnp.float32)
        pair = gains.shape[0]
        partner_gains = (tail[:, :pair] + tail[:, pair:]).T
    else:
        inputs = gathered(projected, "tile", 0)
    earlier = None
    for cycle_index in range(ROUNDS):
        coarse, (solve_now, basis_now, faces_inverse_now) = coarse_of(
            inputs, (local_solve, basis, face_inverse)
        )
        lower_basis = basis_now[lower_at]
        upper_basis = basis_now[upper_at]
        if pairwise and cycle_index == 0:
            sends = jnp.where(
                live,
                jnp.dot(basis_now.T, faces_inverse_now, preferred_element_type=jnp.float32),
                0.0,
            )
            keeps = jnp.where(
                live & live.T,
                jnp.dot(basis_now.T, basis_now, preferred_element_type=jnp.float32),
                0.0,
            )
            mine = jnp.concatenate([sends, keeps], axis=1).astype(jnp.bfloat16)
        coarse = jnp.where(live, coarse, jnp.zeros((), coarse.dtype))
        correction = jnp.dot(basis, coarse, preferred_element_type=jnp.float32)
        iterate = local_solve + correction
        if cycle_index == ROUNDS - 1:
            break
        lower_trace = (
            solve_now[lower_at] + jnp.dot(lower_basis, coarse, preferred_element_type=jnp.float32)
        ).astype(jnp.bfloat16)
        upper_trace = (
            solve_now[upper_at] + jnp.dot(upper_basis, coarse, preferred_element_type=jnp.float32)
        ).astype(jnp.bfloat16)
        rows = lower_trace.shape[0]
        if pairwise:
            toward_partner = jnp.where(first, upper_trace, lower_trace)
            toward_diagonal = jnp.where(first, lower_trace, upper_trace)
            width = toward_partner.shape[1]
            got = swapped(jnp.concatenate([toward_partner, coarse, mine], axis=1), "tile")
            from_diagonal = lax.ppermute(toward_diagonal, DUCT, diagonal_pairs)
            crossing = lax.ppermute(toward_diagonal, DUCT, crossing_pairs)
            from_partner = got[:, :width]
            from_lower = jnp.where(first, from_diagonal, from_partner).astype(jnp.float32)
            from_upper = jnp.where(first, from_partner, from_diagonal).astype(jnp.float32)
            faces = face_rows_of(gains, from_lower, from_upper)
            partner_lower = jnp.where(first, upper_trace, crossing).astype(jnp.float32)
            partner_upper = jnp.where(first, crossing, lower_trace).astype(jnp.float32)
            partner_coarse = got[:, width : 2 * width]
            theirs = got[:, 2 * width :]
            partner_faces = face_rows_of(partner_gains, partner_lower, partner_upper)
            own = projection_of(mine, faces, coarse)
            other = projection_of(theirs, partner_faces, partner_coarse)
            inputs = jnp.concatenate(
                [jnp.where(first, own, other), jnp.where(first, other, own)], axis=0
            )
        else:
            from_lower = passed_along(upper_trace, 1).astype(jnp.float32)
            from_upper = passed_along(lower_trace, -1).astype(jnp.float32)
            faces = face_rows_of(gains, from_lower, from_upper)
        change = jnp.dot(face_inverse, faces, preferred_element_type=jnp.float32)
        local_solve = base_solve + change
        if not pairwise:
            step = change if earlier is None else change - earlier
            inputs = gathered(coarse_input((step - correction).astype(jnp.bfloat16)), "tile", 0)
        earlier = change
    return iterate.astype(jnp.bfloat16)[None]


def solution(mesh):
    placed = (
        P(("group", "sub", "tile"), None, "rep"),
        P(("group", "sub", "tile"), None, None),
        P(("group", "sub", "tile"), None, None),
        P(("group", "sub", "tile"), None, None),
        P(("group", "sub", "tile"), None, None),
        P(("group", "sub", "tile")),
        P("group", "tile", "rep", "sub", None),
    )
    return jax.shard_map(
        local,
        mesh=mesh,
        in_specs=placed,
        out_specs=P(("group", "sub", "tile"), None, "rep"),
        check_vma=False,
    )
```

```python
import jax
import jax.numpy as jnp
from jax import lax
from jax.sharding import PartitionSpec as P

ROUNDS = 2
DUCT = ("sub", "tile")


def passed_along(shard, by):
    peers = lax.axis_size(DUCT)
    pairs = [(i, i + by) for i in range(peers) if 0 <= i + by < peers]
    return lax.ppermute(shard, DUCT, pairs)


def swapped(shard, axis):
    return lax.ppermute(shard, axis, [(0, 1), (1, 0)])


def gathered(shard, axis, dim):
    if lax.axis_size(axis) != 2:
        return lax.all_gather(shard, axis, axis=dim, tiled=True)
    other = swapped(shard, axis)
    first = lax.axis_index(axis) == 0
    return jnp.concatenate(
        [jnp.where(first, shard, other), jnp.where(first, other, shard)], axis=dim
    )


def local(
    right_side,
    interface_inverse,
    coupling,
    trace_rows,
    deflation_basis,
    deflation_counts,
    coarse_inverse,
):
    source = right_side[0]
    inverse = interface_inverse[0]
    iface_rows = inverse.shape[0]
    face_rows = coupling.shape[2]
    slot_count = deflation_basis.shape[2]
    sub_count = lax.axis_size("sub")
    sub_index = lax.axis_index("sub")
    slot_ids = jnp.arange(slot_count, dtype=jnp.int32)
    basis = deflation_basis[0]
    live = (slot_ids < deflation_counts[0])[:, None]
    half_block = coarse_inverse[:, 0, :, 0, :]
    columns = gathered(half_block, "rep", 1)
    lower_gain = coupling[0, 0][:, None]
    upper_gain = coupling[0, 1][:, None]

    lower_at = trace_rows[0, 0]
    upper_at = trace_rows[0, 1]
    face_inverse = jnp.concatenate(
        [inverse[:, :face_rows], inverse[:, iface_rows - face_rows :]], axis=1
    )

    def coarse_input(defect):
        projected = lax.dot_general(
            basis, defect, (((0,), (0,)), ((), ())), preferred_element_type=jnp.float32
        )
        return jnp.where(live, projected, 0.0).astype(jnp.bfloat16)

    def coarse_of(inputs, riders):
        partial = jnp.einsum(
            "jsc,cm->jsm", columns, inputs, preferred_element_type=jnp.float32
        ).astype(jnp.bfloat16)
        partial, riders = lax.optimization_barrier((partial, riders))
        total = lax.dynamic_index_in_dim(partial, sub_index, 0, keepdims=False).astype(
            jnp.float32
        )
        for k in range(1, sub_count):
            piece = lax.dynamic_index_in_dim(partial, (sub_index + k) % sub_count, 0, keepdims=False)
            total = total + lax.ppermute(
                piece, "sub", [(i, (i + k) % sub_count) for i in range(sub_count)]
            ).astype(jnp.float32)
        return total.astype(jnp.bfloat16), riders

    pairwise = lax.axis_size("tile") == 2 and ROUNDS == 2
    tile_index = lax.axis_index("tile")
    gains = coupling[0]
    if pairwise:
        gains_high = gains.T.astype(jnp.bfloat16)
        gains_low = (gains.T - gains_high.astype(jnp.float32)).astype(jnp.bfloat16)
        gains_pair = jnp.concatenate([gains_high, gains_low], axis=1)
        peers = lax.axis_size(DUCT)
        diagonal_pairs = []
        crossing_pairs = []
        for i in range(peers):
            target = i - 1 if i % 2 == 0 else i + 1
            if 0 <= target < peers:
                diagonal_pairs.append((i, target))
            target = i - 2 if i % 2 == 0 else i + 2
            if 0 <= target < peers:
                crossing_pairs.append((i, target))

    def projection_of(mix, faces, coarse):
        return (
            jnp.dot(mix[:, : faces.shape[0]], faces, preferred_element_type=jnp.float32)
            - jnp.dot(mix[:, faces.shape[0] :], coarse, preferred_element_type=jnp.float32)
        ).astype(jnp.bfloat16)

    def face_rows_of(gain, lower, upper):
        return jnp.concatenate(
            [gain[0][:, None] * lower, gain[1][:, None] * upper], axis=0
        ).astype(jnp.bfloat16)

    base_solve = jnp.dot(inverse, source, preferred_element_type=jnp.float32)
    local_solve = base_solve
    projected = coarse_input(local_solve.astype(jnp.bfloat16))
    if pairwise:
        width = projected.shape[1]
        got = swapped(projected, "tile")
        first = tile_index == 0
        inputs = jnp.concatenate(
            [
                jnp.where(first, projected, got[:, :width]),
                jnp.where(first, got[:, :width], projected),
            ],
            axis=0,
        )
    else:
        inputs = gathered(projected, "tile", 0)
    earlier = None
    for cycle_index in range(ROUNDS):
        coarse, (solve_now, basis_now, faces_inverse_now) = coarse_of(
            inputs, (local_solve, basis, face_inverse)
        )
        lower_basis = basis_now[lower_at]
        upper_basis = basis_now[upper_at]
        if pairwise and cycle_index == 0:
            sends = jnp.where(
                live,
                jnp.dot(basis_now.T, faces_inverse_now, preferred_element_type=jnp.float32),
                0.0,
            )
            keeps = jnp.where(
                live & live.T,
                jnp.dot(basis_now.T, basis_now, preferred_element_type=jnp.float32),
                0.0,
            )
            mine = jnp.concatenate([sends, keeps], axis=1).astype(jnp.bfloat16)
        coarse = jnp.where(live, coarse, jnp.zeros((), coarse.dtype))
        correction = jnp.dot(basis, coarse, preferred_element_type=jnp.float32)
        iterate = local_solve + correction
        if cycle_index == ROUNDS - 1:
            break
        lower_trace = (
            solve_now[lower_at] + jnp.dot(lower_basis, coarse, preferred_element_type=jnp.float32)
        ).astype(jnp.bfloat16)
        upper_trace = (
            solve_now[upper_at] + jnp.dot(upper_basis, coarse, preferred_element_type=jnp.float32)
        ).astype(jnp.bfloat16)
        rows = lower_trace.shape[0]
        if pairwise:
            toward_partner = jnp.where(first, upper_trace, lower_trace)
            toward_diagonal = jnp.where(first, lower_trace, upper_trace)
            width = toward_partner.shape[1]
            got = swapped(
                jnp.concatenate([toward_partner, coarse, mine, gains_pair], axis=1), "tile"
            )
            from_diagonal = lax.ppermute(toward_diagonal, DUCT, diagonal_pairs)
            crossing = lax.ppermute(toward_diagonal, DUCT, crossing_pairs)
            from_partner = got[:, :width]
            from_lower = jnp.where(first, from_diagonal, from_partner).astype(jnp.float32)
            from_upper = jnp.where(first, from_partner, from_diagonal).astype(jnp.float32)
            faces = face_rows_of(gains, from_lower, from_upper)
            partner_lower = jnp.where(first, upper_trace, crossing).astype(jnp.float32)
            partner_upper = jnp.where(first, crossing, lower_trace).astype(jnp.float32)
            partner_coarse = got[:, width : 2 * width]
            theirs = got[:, 2 * width : 2 * width + mine.shape[1]]
            tail = got[:, 2 * width + mine.shape[1] :].astype(jnp.float32)
            pair = gains.shape[0]
            partner_gains = (tail[:, :pair] + tail[:, pair:]).T
            partner_faces = face_rows_of(partner_gains, partner_lower, partner_upper)
            own = projection_of(mine, faces, coarse)
            other = projection_of(theirs, partner_faces, partner_coarse)
            inputs = jnp.concatenate(
                [jnp.where(first, own, other), jnp.where(first, other, own)], axis=0
            )
        else:
            from_lower = passed_along(upper_trace, 1).astype(jnp.float32)
            from_upper = passed_along(lower_trace, -1).astype(jnp.float32)
            faces = face_rows_of(gains, from_lower, from_upper)
        change = jnp.dot(face_inverse, faces, preferred_element_type=jnp.float32)
        local_solve = base_solve + change
        if not pairwise:
            step = change if earlier is None else change - earlier
            inputs = gathered(coarse_input((step - correction).astype(jnp.bfloat16)), "tile", 0)
        earlier = change
    return iterate.astype(jnp.bfloat16)[None]


def solution(mesh):
    placed = (
        P(("group", "sub", "tile"), None, "rep"),
        P(("group", "sub", "tile"), None, None),
        P(("group", "sub", "tile"), None, None),
        P(("group", "sub", "tile"), None, None),
        P(("group", "sub", "tile"), None, None),
        P(("group", "sub", "tile")),
        P("group", "tile", "rep", "sub", None),
    )
    return jax.shard_map(
        local,
        mesh=mesh,
        in_specs=placed,
        out_specs=P(("group", "sub", "tile"), None, "rep"),
        check_vma=False,
    )
```

```python
import jax
import jax.numpy as jnp
from jax import lax
from jax.sharding import PartitionSpec as P

ROUNDS = 2
DUCT = ("sub", "tile")


def passed_along(shard, by):
    peers = lax.axis_size(DUCT)
    pairs = [(i, i + by) for i in range(peers) if 0 <= i + by < peers]
    return lax.ppermute(shard, DUCT, pairs)


def swapped(shard, axis):
    return lax.ppermute(shard, axis, [(0, 1), (1, 0)])


def gathered(shard, axis, dim):
    if lax.axis_size(axis) != 2:
        return lax.all_gather(shard, axis, axis=dim, tiled=True)
    other = swapped(shard, axis)
    first = lax.axis_index(axis) == 0
    return jnp.concatenate(
        [jnp.where(first, shard, other), jnp.where(first, other, shard)], axis=dim
    )


def local(
    right_side,
    interface_inverse,
    coupling,
    trace_rows,
    deflation_basis,
    deflation_counts,
    coarse_inverse,
):
    source = right_side[0]
    inverse = interface_inverse[0]
    iface_rows = inverse.shape[0]
    face_rows = coupling.shape[2]
    slot_count = deflation_basis.shape[2]
    sub_count = lax.axis_size("sub")
    sub_index = lax.axis_index("sub")
    slot_ids = jnp.arange(slot_count, dtype=jnp.int32)
    basis = deflation_basis[0]
    live = (slot_ids < deflation_counts[0])[:, None]
    half_block = coarse_inverse[:, 0, :, 0, :]
    columns = gathered(half_block, "rep", 1)
    lower_gain = coupling[0, 0][:, None]
    upper_gain = coupling[0, 1][:, None]

    lower_at = trace_rows[0, 0]
    upper_at = trace_rows[0, 1]
    face_inverse = jnp.concatenate(
        [inverse[:, :face_rows], inverse[:, iface_rows - face_rows :]], axis=1
    )

    def coarse_input(defect):
        projected = lax.dot_general(
            basis, defect, (((0,), (0,)), ((), ())), preferred_element_type=jnp.float32
        )
        return jnp.where(live, projected, 0.0).astype(jnp.bfloat16)

    def coarse_of(inputs, riders):
        partial = jnp.einsum(
            "jsc,cm->jsm", columns, inputs, preferred_element_type=jnp.float32
        ).astype(jnp.bfloat16)
        partial, riders = lax.optimization_barrier((partial, riders))
        total = lax.dynamic_index_in_dim(partial, sub_index, 0, keepdims=False).astype(
            jnp.float32
        )
        for k in range(1, sub_count):
            piece = lax.dynamic_index_in_dim(partial, (sub_index + k) % sub_count, 0, keepdims=False)
            total = total + lax.ppermute(
                piece, "sub", [(i, (i + k) % sub_count) for i in range(sub_count)]
            ).astype(jnp.float32)
        return total.astype(jnp.bfloat16), riders

    pairwise = lax.axis_size("tile") == 2 and ROUNDS == 2
    tile_index = lax.axis_index("tile")
    gains = coupling[0]
    if pairwise:
        gains_high = gains.T.astype(jnp.bfloat16)
        gains_low = (gains.T - gains_high.astype(jnp.float32)).astype(jnp.bfloat16)
        gains_pair = jnp.concatenate([gains_high, gains_low], axis=1)
        peers = lax.axis_size(DUCT)
        diagonal_pairs = []
        crossing_pairs = []
        for i in range(peers):
            target = i - 1 if i % 2 == 0 else i + 1
            if 0 <= target < peers:
                diagonal_pairs.append((i, target))
            target = i - 2 if i % 2 == 0 else i + 2
            if 0 <= target < peers:
                crossing_pairs.append((i, target))

    def projection_of(mix, faces, coarse):
        return (
            jnp.dot(mix[:, : faces.shape[0]], faces, preferred_element_type=jnp.float32)
            - jnp.dot(mix[:, faces.shape[0] :], coarse, preferred_element_type=jnp.float32)
        ).astype(jnp.bfloat16)

    def face_rows_of(gain, lower, upper):
        return jnp.concatenate(
            [gain[0][:, None] * lower, gain[1][:, None] * upper], axis=0
        ).astype(jnp.bfloat16)

    base_solve = jnp.dot(inverse, source, preferred_element_type=jnp.float32)
    local_solve = base_solve
    projected = coarse_input(local_solve.astype(jnp.bfloat16))
    if pairwise:
        width = projected.shape[1]
        got = swapped(projected, "tile")
        first = tile_index == 0
        inputs = jnp.concatenate(
            [
                jnp.where(first, projected, got[:, :width]),
                jnp.where(first, got[:, :width], projected),
            ],
            axis=0,
        )
    else:
        inputs = gathered(projected, "tile", 0)
    earlier = None
    for cycle_index in range(ROUNDS):
        coarse, (solve_now, basis_now, faces_inverse_now) = coarse_of(
            inputs, (local_solve, basis, face_inverse)
        )
        trace_at = jnp.concatenate([lower_at, upper_at])
        trace_basis = jnp.take(basis_now, trace_at, axis=0)
        trace_solve = jnp.take(solve_now, trace_at, axis=0)
        if pairwise and cycle_index == 0:
            sends = jnp.where(
                live,
                jnp.dot(basis_now.T, faces_inverse_now, preferred_element_type=jnp.float32),
                0.0,
            )
            keeps = jnp.where(
                live & live.T,
                jnp.dot(basis_now.T, basis_now, preferred_element_type=jnp.float32),
                0.0,
            )
            mine = jnp.concatenate([sends, keeps], axis=1).astype(jnp.bfloat16)
        coarse = jnp.where(live, coarse, jnp.zeros((), coarse.dtype))
        correction = jnp.dot(basis, coarse, preferred_element_type=jnp.float32)
        iterate = local_solve + correction
        if cycle_index == ROUNDS - 1:
            break
        traces = (
            trace_solve + jnp.dot(trace_basis, coarse, preferred_element_type=jnp.float32)
        ).astype(jnp.bfloat16)
        rows = lower_at.shape[0]
        lower_trace = traces[:rows]
        upper_trace = traces[rows:]
        if pairwise:
            toward_partner = jnp.where(first, upper_trace, lower_trace)
            toward_diagonal = jnp.where(first, lower_trace, upper_trace)
            width = toward_partner.shape[1]
            got = swapped(
                jnp.concatenate([toward_partner, coarse, mine, gains_pair], axis=1), "tile"
            )
            from_diagonal = lax.ppermute(toward_diagonal, DUCT, diagonal_pairs)
            crossing = lax.ppermute(toward_diagonal, DUCT, crossing_pairs)
            from_partner = got[:, :width]
            from_lower = jnp.where(first, from_diagonal, from_partner).astype(jnp.float32)
            from_upper = jnp.where(first, from_partner, from_diagonal).astype(jnp.float32)
            faces = face_rows_of(gains, from_lower, from_upper)
            partner_lower = jnp.where(first, upper_trace, crossing).astype(jnp.float32)
            partner_upper = jnp.where(first, crossing, lower_trace).astype(jnp.float32)
            partner_coarse = got[:, width : 2 * width]
            theirs = got[:, 2 * width : 2 * width + mine.shape[1]]
            tail = got[:, 2 * width + mine.shape[1] :].astype(jnp.float32)
            pair = gains.shape[0]
            partner_gains = (tail[:, :pair] + tail[:, pair:]).T
            partner_faces = face_rows_of(partner_gains, partner_lower, partner_upper)
            own = projection_of(mine, faces, coarse)
            other = projection_of(theirs, partner_faces, partner_coarse)
            inputs = jnp.concatenate(
                [jnp.where(first, own, other), jnp.where(first, other, own)], axis=0
            )
        else:
            from_lower = passed_along(upper_trace, 1).astype(jnp.float32)
            from_upper = passed_along(lower_trace, -1).astype(jnp.float32)
            faces = face_rows_of(gains, from_lower, from_upper)
        change = jnp.dot(face_inverse, faces, preferred_element_type=jnp.float32)
        local_solve = base_solve + change
        if not pairwise:
            step = change if earlier is None else change - earlier
            inputs = gathered(coarse_input((step - correction).astype(jnp.bfloat16)), "tile", 0)
        earlier = change
    return iterate.astype(jnp.bfloat16)[None]


def solution(mesh):
    placed = (
        P(("group", "sub", "tile"), None, "rep"),
        P(("group", "sub", "tile"), None, None),
        P(("group", "sub", "tile"), None, None),
        P(("group", "sub", "tile"), None, None),
        P(("group", "sub", "tile"), None, None),
        P(("group", "sub", "tile")),
        P("group", "tile", "rep", "sub", None),
    )
    return jax.shard_map(
        local,
        mesh=mesh,
        in_specs=placed,
        out_specs=P(("group", "sub", "tile"), None, "rep"),
        check_vma=False,
    )
```

```python
import jax
import jax.numpy as jnp
from jax import lax
from jax.sharding import PartitionSpec as P

ROUNDS = 2
DUCT = ("sub", "tile")


def passed_along(shard, by):
    peers = lax.axis_size(DUCT)
    pairs = [(i, i + by) for i in range(peers) if 0 <= i + by < peers]
    return lax.ppermute(shard, DUCT, pairs)


def swapped(shard, axis):
    return lax.ppermute(shard, axis, [(0, 1), (1, 0)])


def gathered(shard, axis, dim):
    if lax.axis_size(axis) != 2:
        return lax.all_gather(shard, axis, axis=dim, tiled=True)
    other = swapped(shard, axis)
    first = lax.axis_index(axis) == 0
    return jnp.concatenate(
        [jnp.where(first, shard, other), jnp.where(first, other, shard)], axis=dim
    )


def local(
    right_side,
    interface_inverse,
    coupling,
    trace_rows,
    deflation_basis,
    deflation_counts,
    coarse_inverse,
):
    source = right_side[0]
    inverse = interface_inverse[0]
    iface_rows = inverse.shape[0]
    face_rows = coupling.shape[2]
    slot_count = deflation_basis.shape[2]
    sub_count = lax.axis_size("sub")
    sub_index = lax.axis_index("sub")
    slot_ids = jnp.arange(slot_count, dtype=jnp.int32)
    basis = deflation_basis[0]
    live = (slot_ids < deflation_counts[0])[:, None]
    half_block = coarse_inverse[:, 0, :, 0, :]
    columns = gathered(half_block, "rep", 1)
    lower_gain = coupling[0, 0][:, None]
    upper_gain = coupling[0, 1][:, None]

    lower_at = trace_rows[0, 0]
    upper_at = trace_rows[0, 1]
    face_inverse = jnp.concatenate(
        [inverse[:, :face_rows], inverse[:, iface_rows - face_rows :]], axis=1
    )

    def coarse_input(defect):
        projected = lax.dot_general(
            basis, defect, (((0,), (0,)), ((), ())), preferred_element_type=jnp.float32
        )
        return jnp.where(live, projected, 0.0).astype(jnp.bfloat16)

    def coarse_of(inputs, riders):
        partial = jnp.einsum(
            "jsc,cm->jsm", columns, inputs, preferred_element_type=jnp.float32
        ).astype(jnp.bfloat16)
        partial, riders = lax.optimization_barrier((partial, riders))
        total = lax.dynamic_index_in_dim(partial, sub_index, 0, keepdims=False).astype(
            jnp.float32
        )
        for k in range(1, sub_count):
            piece = lax.dynamic_index_in_dim(partial, (sub_index + k) % sub_count, 0, keepdims=False)
            total = total + lax.ppermute(
                piece, "sub", [(i, (i + k) % sub_count) for i in range(sub_count)]
            ).astype(jnp.float32)
        return total.astype(jnp.bfloat16), riders

    pairwise = lax.axis_size("tile") == 2 and ROUNDS == 2
    tile_index = lax.axis_index("tile")
    gains = coupling[0]
    if pairwise:
        gains_high = gains.T.astype(jnp.bfloat16)
        gains_low = (gains.T - gains_high.astype(jnp.float32)).astype(jnp.bfloat16)
        gains_pair = jnp.concatenate([gains_high, gains_low], axis=1)
        peers = lax.axis_size(DUCT)
        diagonal_pairs = []
        crossing_pairs = []
        for i in range(peers):
            target = i - 1 if i % 2 == 0 else i + 1
            if 0 <= target < peers:
                diagonal_pairs.append((i, target))
            target = i - 2 if i % 2 == 0 else i + 2
            if 0 <= target < peers:
                crossing_pairs.append((i, target))

    def projection_of(mix, faces, coarse):
        return (
            jnp.dot(mix[:, : faces.shape[0]], faces, preferred_element_type=jnp.float32)
            - jnp.dot(mix[:, faces.shape[0] :], coarse, preferred_element_type=jnp.float32)
        ).astype(jnp.bfloat16)

    def face_rows_of(gain, lower, upper):
        return jnp.concatenate(
            [gain[0][:, None] * lower, gain[1][:, None] * upper], axis=0
        ).astype(jnp.bfloat16)

    base_solve = jnp.dot(inverse, source, preferred_element_type=jnp.float32)
    local_solve = base_solve
    projected = coarse_input(local_solve.astype(jnp.bfloat16))
    if pairwise:
        width = projected.shape[1]
        got = swapped(projected, "tile")
        first = tile_index == 0
        inputs = jnp.concatenate(
            [
                jnp.where(first, projected, got[:, :width]),
                jnp.where(first, got[:, :width], projected),
            ],
            axis=0,
        )
    else:
        inputs = gathered(projected, "tile", 0)
    earlier = None
    for cycle_index in range(ROUNDS):
        coarse, (solve_now, basis_now, faces_inverse_now) = coarse_of(
            inputs, (local_solve, basis, face_inverse)
        )
        lower_basis = basis_now[lower_at]
        upper_basis = basis_now[upper_at]
        if pairwise and cycle_index == 0:
            sends = jnp.where(
                live,
                jnp.dot(basis_now.T, faces_inverse_now, preferred_element_type=jnp.float32),
                0.0,
            )
            keeps = jnp.where(
                live & live.T,
                jnp.dot(basis_now.T, basis_now, preferred_element_type=jnp.float32),
                0.0,
            )
            mine = jnp.concatenate([sends, keeps], axis=1).astype(jnp.bfloat16)
            got_once = swapped(jnp.concatenate([mine, gains_pair], axis=1), "tile")
            theirs = got_once[:, : mine.shape[1]]
            tail = got_once[:, mine.shape[1] :].astype(jnp.float32)
            pair = gains.shape[0]
            partner_gains = (tail[:, :pair] + tail[:, pair:]).T
        coarse = jnp.where(live, coarse, jnp.zeros((), coarse.dtype))
        correction = jnp.dot(basis, coarse, preferred_element_type=jnp.float32)
        iterate = local_solve + correction
        if cycle_index == ROUNDS - 1:
            break
        lower_trace = (
            solve_now[lower_at] + jnp.dot(lower_basis, coarse, preferred_element_type=jnp.float32)
        ).astype(jnp.bfloat16)
        upper_trace = (
            solve_now[upper_at] + jnp.dot(upper_basis, coarse, preferred_element_type=jnp.float32)
        ).astype(jnp.bfloat16)
        rows = lower_trace.shape[0]
        if pairwise:
            toward_partner = jnp.where(first, upper_trace, lower_trace)
            toward_diagonal = jnp.where(first, lower_trace, upper_trace)
            width = toward_partner.shape[1]
            got = swapped(jnp.concatenate([toward_partner, coarse], axis=1), "tile")
            from_diagonal = lax.ppermute(toward_diagonal, DUCT, diagonal_pairs)
            crossing = lax.ppermute(toward_diagonal, DUCT, crossing_pairs)
            from_partner = got[:, :width]
            from_lower = jnp.where(first, from_diagonal, from_partner).astype(jnp.float32)
            from_upper = jnp.where(first, from_partner, from_diagonal).astype(jnp.float32)
            faces = face_rows_of(gains, from_lower, from_upper)
            partner_lower = jnp.where(first, upper_trace, crossing).astype(jnp.float32)
            partner_upper = jnp.where(first, crossing, lower_trace).astype(jnp.float32)
            partner_coarse = got[:, width : 2 * width]
            partner_faces = face_rows_of(partner_gains, partner_lower, partner_upper)
            own = projection_of(mine, faces, coarse)
            other = projection_of(theirs, partner_faces, partner_coarse)
            inputs = jnp.concatenate(
                [jnp.where(first, own, other), jnp.where(first, other, own)], axis=0
            )
        else:
            from_lower = passed_along(upper_trace, 1).astype(jnp.float32)
            from_upper = passed_along(lower_trace, -1).astype(jnp.float32)
            faces = face_rows_of(gains, from_lower, from_upper)
        change = jnp.dot(face_inverse, faces, preferred_element_type=jnp.float32)
        local_solve = base_solve + change
        if not pairwise:
            step = change if earlier is None else change - earlier
            inputs = gathered(coarse_input((step - correction).astype(jnp.bfloat16)), "tile", 0)
        earlier = change
    return iterate.astype(jnp.bfloat16)[None]


def solution(mesh):
    placed = (
        P(("group", "sub", "tile"), None, "rep"),
        P(("group", "sub", "tile"), None, None),
        P(("group", "sub", "tile"), None, None),
        P(("group", "sub", "tile"), None, None),
        P(("group", "sub", "tile"), None, None),
        P(("group", "sub", "tile")),
        P("group", "tile", "rep", "sub", None),
    )
    return jax.shard_map(
        local,
        mesh=mesh,
        in_specs=placed,
        out_specs=P(("group", "sub", "tile"), None, "rep"),
        check_vma=False,
    )
```

```python
import jax
import jax.numpy as jnp
from jax import lax
from jax.sharding import PartitionSpec as P

ROUNDS = 2
DUCT = ("sub", "tile")


def passed_along(shard, by):
    peers = lax.axis_size(DUCT)
    pairs = [(i, i + by) for i in range(peers) if 0 <= i + by < peers]
    return lax.ppermute(shard, DUCT, pairs)


def swapped(shard, axis):
    return lax.ppermute(shard, axis, [(0, 1), (1, 0)])


def gathered(shard, axis, dim):
    if lax.axis_size(axis) != 2:
        return lax.all_gather(shard, axis, axis=dim, tiled=True)
    other = swapped(shard, axis)
    first = lax.axis_index(axis) == 0
    return jnp.concatenate(
        [jnp.where(first, shard, other), jnp.where(first, other, shard)], axis=dim
    )


def local(
    right_side,
    interface_inverse,
    coupling,
    trace_rows,
    deflation_basis,
    deflation_counts,
    coarse_inverse,
):
    source = right_side[0]
    inverse = interface_inverse[0]
    iface_rows = inverse.shape[0]
    face_rows = coupling.shape[2]
    slot_count = deflation_basis.shape[2]
    sub_count = lax.axis_size("sub")
    sub_index = lax.axis_index("sub")
    slot_ids = jnp.arange(slot_count, dtype=jnp.int32)
    basis = deflation_basis[0]
    live = (slot_ids < deflation_counts[0])[:, None]
    half_block = coarse_inverse[:, 0, :, 0, :]
    columns = gathered(half_block, "rep", 1)
    lower_gain = coupling[0, 0][:, None]
    upper_gain = coupling[0, 1][:, None]

    lower_at = trace_rows[0, 0]
    upper_at = trace_rows[0, 1]
    face_inverse = jnp.concatenate(
        [inverse[:, :face_rows], inverse[:, iface_rows - face_rows :]], axis=1
    )

    def coarse_input(defect):
        projected = lax.dot_general(
            basis, defect, (((0,), (0,)), ((), ())), preferred_element_type=jnp.float32
        )
        return jnp.where(live, projected, 0.0).astype(jnp.bfloat16)

    def coarse_of(inputs, riders):
        partial = jnp.einsum(
            "jsc,cm->jsm", columns, inputs, preferred_element_type=jnp.float32
        ).astype(jnp.bfloat16)
        partial, riders = lax.optimization_barrier((partial, riders))
        arrived = lax.all_to_all(partial, "sub", split_axis=0, concat_axis=0, tiled=True)
        total = jnp.sum(arrived.astype(jnp.float32), axis=0)
        return total.astype(jnp.bfloat16), riders

    pairwise = lax.axis_size("tile") == 2 and ROUNDS == 2
    tile_index = lax.axis_index("tile")
    gains = coupling[0]
    if pairwise:
        gains_high = gains.T.astype(jnp.bfloat16)
        gains_low = (gains.T - gains_high.astype(jnp.float32)).astype(jnp.bfloat16)
        gains_pair = jnp.concatenate([gains_high, gains_low], axis=1)
        peers = lax.axis_size(DUCT)
        diagonal_pairs = []
        crossing_pairs = []
        for i in range(peers):
            target = i - 1 if i % 2 == 0 else i + 1
            if 0 <= target < peers:
                diagonal_pairs.append((i, target))
            target = i - 2 if i % 2 == 0 else i + 2
            if 0 <= target < peers:
                crossing_pairs.append((i, target))

    def projection_of(mix, faces, coarse):
        return (
            jnp.dot(mix[:, : faces.shape[0]], faces, preferred_element_type=jnp.float32)
            - jnp.dot(mix[:, faces.shape[0] :], coarse, preferred_element_type=jnp.float32)
        ).astype(jnp.bfloat16)

    def face_rows_of(gain, lower, upper):
        return jnp.concatenate(
            [gain[0][:, None] * lower, gain[1][:, None] * upper], axis=0
        ).astype(jnp.bfloat16)

    base_solve = jnp.dot(inverse, source, preferred_element_type=jnp.float32)
    local_solve = base_solve
    projected = coarse_input(local_solve.astype(jnp.bfloat16))
    if pairwise:
        width = projected.shape[1]
        got = swapped(projected, "tile")
        first = tile_index == 0
        inputs = jnp.concatenate(
            [
                jnp.where(first, projected, got[:, :width]),
                jnp.where(first, got[:, :width], projected),
            ],
            axis=0,
        )
    else:
        inputs = gathered(projected, "tile", 0)
    earlier = None
    for cycle_index in range(ROUNDS):
        coarse, (solve_now, basis_now, faces_inverse_now) = coarse_of(
            inputs, (local_solve, basis, face_inverse)
        )
        lower_basis = basis_now[lower_at]
        upper_basis = basis_now[upper_at]
        if pairwise and cycle_index == 0:
            sends = jnp.where(
                live,
                jnp.dot(basis_now.T, faces_inverse_now, preferred_element_type=jnp.float32),
                0.0,
            )
            keeps = jnp.where(
                live & live.T,
                jnp.dot(basis_now.T, basis_now, preferred_element_type=jnp.float32),
                0.0,
            )
            mine = jnp.concatenate([sends, keeps], axis=1).astype(jnp.bfloat16)
        coarse = jnp.where(live, coarse, jnp.zeros((), coarse.dtype))
        correction = jnp.dot(basis, coarse, preferred_element_type=jnp.float32)
        iterate = local_solve + correction
        if cycle_index == ROUNDS - 1:
            break
        lower_trace = (
            solve_now[lower_at] + jnp.dot(lower_basis, coarse, preferred_element_type=jnp.float32)
        ).astype(jnp.bfloat16)
        upper_trace = (
            solve_now[upper_at] + jnp.dot(upper_basis, coarse, preferred_element_type=jnp.float32)
        ).astype(jnp.bfloat16)
        rows = lower_trace.shape[0]
        if pairwise:
            toward_partner = jnp.where(first, upper_trace, lower_trace)
            toward_diagonal = jnp.where(first, lower_trace, upper_trace)
            width = toward_partner.shape[1]
            got = swapped(
                jnp.concatenate([toward_partner, coarse, mine, gains_pair], axis=1), "tile"
            )
            from_diagonal = lax.ppermute(toward_diagonal, DUCT, diagonal_pairs)
            crossing = lax.ppermute(toward_diagonal, DUCT, crossing_pairs)
            from_partner = got[:, :width]
            from_lower = jnp.where(first, from_diagonal, from_partner).astype(jnp.float32)
            from_upper = jnp.where(first, from_partner, from_diagonal).astype(jnp.float32)
            faces = face_rows_of(gains, from_lower, from_upper)
            partner_lower = jnp.where(first, upper_trace, crossing).astype(jnp.float32)
            partner_upper = jnp.where(first, crossing, lower_trace).astype(jnp.float32)
            partner_coarse = got[:, width : 2 * width]
            theirs = got[:, 2 * width : 2 * width + mine.shape[1]]
            tail = got[:, 2 * width + mine.shape[1] :].astype(jnp.float32)
            pair = gains.shape[0]
            partner_gains = (tail[:, :pair] + tail[:, pair:]).T
            partner_faces = face_rows_of(partner_gains, partner_lower, partner_upper)
            own = projection_of(mine, faces, coarse)
            other = projection_of(theirs, partner_faces, partner_coarse)
            inputs = jnp.concatenate(
                [jnp.where(first, own, other), jnp.where(first, other, own)], axis=0
            )
        else:
            from_lower = passed_along(upper_trace, 1).astype(jnp.float32)
            from_upper = passed_along(lower_trace, -1).astype(jnp.float32)
            faces = face_rows_of(gains, from_lower, from_upper)
        change = jnp.dot(face_inverse, faces, preferred_element_type=jnp.float32)
        local_solve = base_solve + change
        if not pairwise:
            step = change if earlier is None else change - earlier
            inputs = gathered(coarse_input((step - correction).astype(jnp.bfloat16)), "tile", 0)
        earlier = change
    return iterate.astype(jnp.bfloat16)[None]


def solution(mesh):
    placed = (
        P(("group", "sub", "tile"), None, "rep"),
        P(("group", "sub", "tile"), None, None),
        P(("group", "sub", "tile"), None, None),
        P(("group", "sub", "tile"), None, None),
        P(("group", "sub", "tile"), None, None),
        P(("group", "sub", "tile")),
        P("group", "tile", "rep", "sub", None),
    )
    return jax.shard_map(
        local,
        mesh=mesh,
        in_specs=placed,
        out_specs=P(("group", "sub", "tile"), None, "rep"),
        check_vma=False,
    )
```

```python
import jax
import jax.numpy as jnp
from jax import lax
from jax.sharding import PartitionSpec as P

ROUNDS = 2
DUCT = ("sub", "tile")


def passed_along(shard, by):
    peers = lax.axis_size(DUCT)
    pairs = [(i, i + by) for i in range(peers) if 0 <= i + by < peers]
    return lax.ppermute(shard, DUCT, pairs)


def swapped(shard, axis):
    return lax.ppermute(shard, axis, [(0, 1), (1, 0)])


def gathered(shard, axis, dim):
    if lax.axis_size(axis) != 2:
        return lax.all_gather(shard, axis, axis=dim, tiled=True)
    other = swapped(shard, axis)
    first = lax.axis_index(axis) == 0
    return jnp.concatenate(
        [jnp.where(first, shard, other), jnp.where(first, other, shard)], axis=dim
    )


def local(
    right_side,
    interface_inverse,
    coupling,
    trace_rows,
    deflation_basis,
    deflation_counts,
    coarse_inverse,
):
    source = right_side[0]
    inverse = interface_inverse[0]
    iface_rows = inverse.shape[0]
    face_rows = coupling.shape[2]
    slot_count = deflation_basis.shape[2]
    sub_count = lax.axis_size("sub")
    sub_index = lax.axis_index("sub")
    slot_ids = jnp.arange(slot_count, dtype=jnp.int32)
    basis = deflation_basis[0]
    live = (slot_ids < deflation_counts[0])[:, None]
    half_block = coarse_inverse[:, 0, :, 0, :]
    columns = gathered(half_block, "rep", 1)
    lower_gain = coupling[0, 0][:, None]
    upper_gain = coupling[0, 1][:, None]

    lower_at = trace_rows[0, 0]
    upper_at = trace_rows[0, 1]
    face_inverse = jnp.concatenate(
        [inverse[:, :face_rows], inverse[:, iface_rows - face_rows :]], axis=1
    )

    def coarse_input(defect):
        projected = lax.dot_general(
            basis, defect, (((0,), (0,)), ((), ())), preferred_element_type=jnp.float32
        )
        return jnp.where(live, projected, 0.0).astype(jnp.bfloat16)

    def coarse_of(inputs, riders):
        partial = jnp.einsum(
            "jsc,cm->jsm", columns, inputs, preferred_element_type=jnp.float32
        ).astype(jnp.bfloat16)
        partial, riders = lax.optimization_barrier((partial, riders))
        total = lax.dynamic_index_in_dim(partial, sub_index, 0, keepdims=False).astype(
            jnp.float32
        )
        for k in range(1, sub_count):
            piece = lax.dynamic_index_in_dim(partial, (sub_index + k) % sub_count, 0, keepdims=False)
            total = total + lax.ppermute(
                piece, "sub", [(i, (i + k) % sub_count) for i in range(sub_count)]
            ).astype(jnp.float32)
        return total.astype(jnp.bfloat16), riders

    pairwise = lax.axis_size("tile") == 2 and ROUNDS == 2
    tile_index = lax.axis_index("tile")
    gains = coupling[0]
    if pairwise:
        gains_high = gains.T.astype(jnp.bfloat16)
        gains_low = (gains.T - gains_high.astype(jnp.float32)).astype(jnp.bfloat16)
        gains_pair = jnp.concatenate([gains_high, gains_low], axis=1)
        peers = lax.axis_size(DUCT)
        diagonal_pairs = []
        crossing_pairs = []
        for i in range(peers):
            target = i - 1 if i % 2 == 0 else i + 1
            if 0 <= target < peers:
                diagonal_pairs.append((i, target))
            target = i - 2 if i % 2 == 0 else i + 2
            if 0 <= target < peers:
                crossing_pairs.append((i, target))

    def projection_of(mix, faces, coarse):
        half = mix.shape[1] // 2
        total = 0.0
        for part in (mix[:, :half], mix[:, half:]):
            total = total + (
                jnp.dot(part[:, : faces.shape[0]], faces, preferred_element_type=jnp.float32)
                - jnp.dot(part[:, faces.shape[0] :], coarse, preferred_element_type=jnp.float32)
            )
        return total.astype(jnp.bfloat16)

    def face_rows_of(gain, lower, upper):
        return jnp.concatenate(
            [gain[0][:, None] * lower, gain[1][:, None] * upper], axis=0
        ).astype(jnp.bfloat16)

    base_solve = jnp.dot(inverse, source, preferred_element_type=jnp.float32)
    local_solve = base_solve
    projected = coarse_input(local_solve.astype(jnp.bfloat16))
    if pairwise:
        width = projected.shape[1]
        got = swapped(projected, "tile")
        first = tile_index == 0
        inputs = jnp.concatenate(
            [
                jnp.where(first, projected, got[:, :width]),
                jnp.where(first, got[:, :width], projected),
            ],
            axis=0,
        )
    else:
        inputs = gathered(projected, "tile", 0)
    earlier = None
    for cycle_index in range(ROUNDS):
        coarse, (solve_now, basis_now, faces_inverse_now) = coarse_of(
            inputs, (local_solve, basis, face_inverse)
        )
        lower_basis = basis_now[lower_at]
        upper_basis = basis_now[upper_at]
        if pairwise and cycle_index == 0:
            sends = jnp.where(
                live,
                jnp.dot(basis_now.T, faces_inverse_now, preferred_element_type=jnp.float32),
                0.0,
            )
            keeps = jnp.where(
                live & live.T,
                jnp.dot(basis_now.T, basis_now, preferred_element_type=jnp.float32),
                0.0,
            )
            exact = jnp.concatenate([sends, keeps], axis=1)
            high = exact.astype(jnp.bfloat16)
            low = (exact - high.astype(jnp.float32)).astype(jnp.bfloat16)
            mine = jnp.concatenate([high, low], axis=1)
        coarse = jnp.where(live, coarse, jnp.zeros((), coarse.dtype))
        correction = jnp.dot(basis, coarse, preferred_element_type=jnp.float32)
        iterate = local_solve + correction
        if cycle_index == ROUNDS - 1:
            break
        lower_trace = (
            solve_now[lower_at] + jnp.dot(lower_basis, coarse, preferred_element_type=jnp.float32)
        ).astype(jnp.bfloat16)
        upper_trace = (
            solve_now[upper_at] + jnp.dot(upper_basis, coarse, preferred_element_type=jnp.float32)
        ).astype(jnp.bfloat16)
        rows = lower_trace.shape[0]
        if pairwise:
            toward_partner = jnp.where(first, upper_trace, lower_trace)
            toward_diagonal = jnp.where(first, lower_trace, upper_trace)
            width = toward_partner.shape[1]
            got = swapped(
                jnp.concatenate([toward_partner, coarse, mine, gains_pair], axis=1), "tile"
            )
            from_diagonal = lax.ppermute(toward_diagonal, DUCT, diagonal_pairs)
            crossing = lax.ppermute(toward_diagonal, DUCT, crossing_pairs)
            from_partner = got[:, :width]
            from_lower = jnp.where(first, from_diagonal, from_partner).astype(jnp.float32)
            from_upper = jnp.where(first, from_partner, from_diagonal).astype(jnp.float32)
            faces = face_rows_of(gains, from_lower, from_upper)
            partner_lower = jnp.where(first, upper_trace, crossing).astype(jnp.float32)
            partner_upper = jnp.where(first, crossing, lower_trace).astype(jnp.float32)
            partner_coarse = got[:, width : 2 * width]
            theirs = got[:, 2 * width : 2 * width + mine.shape[1]]
            tail = got[:, 2 * width + mine.shape[1] :].astype(jnp.float32)
            pair = gains.shape[0]
            partner_gains = (tail[:, :pair] + tail[:, pair:]).T
            partner_faces = face_rows_of(partner_gains, partner_lower, partner_upper)
            own = projection_of(mine, faces, coarse)
            other = projection_of(theirs, partner_faces, partner_coarse)
            inputs = jnp.concatenate(
                [jnp.where(first, own, other), jnp.where(first, other, own)], axis=0
            )
        else:
            from_lower = passed_along(upper_trace, 1).astype(jnp.float32)
            from_upper = passed_along(lower_trace, -1).astype(jnp.float32)
            faces = face_rows_of(gains, from_lower, from_upper)
        change = jnp.dot(face_inverse, faces, preferred_element_type=jnp.float32)
        local_solve = base_solve + change
        if not pairwise:
            step = change if earlier is None else change - earlier
            inputs = gathered(coarse_input((step - correction).astype(jnp.bfloat16)), "tile", 0)
        earlier = change
    return iterate.astype(jnp.bfloat16)[None]


def solution(mesh):
    placed = (
        P(("group", "sub", "tile"), None, "rep"),
        P(("group", "sub", "tile"), None, None),
        P(("group", "sub", "tile"), None, None),
        P(("group", "sub", "tile"), None, None),
        P(("group", "sub", "tile"), None, None),
        P(("group", "sub", "tile")),
        P("group", "tile", "rep", "sub", None),
    )
    return jax.shard_map(
        local,
        mesh=mesh,
        in_specs=placed,
        out_specs=P(("group", "sub", "tile"), None, "rep"),
        check_vma=False,
    )
```

```python
import jax
import jax.numpy as jnp
from jax import lax
from jax.sharding import PartitionSpec as P

ROUNDS = 2
DUCT = ("sub", "tile")


def passed_along(shard, by):
    peers = lax.axis_size(DUCT)
    pairs = [(i, i + by) for i in range(peers) if 0 <= i + by < peers]
    return lax.ppermute(shard, DUCT, pairs)


def swapped(shard, axis):
    return lax.ppermute(shard, axis, [(0, 1), (1, 0)])


def gathered(shard, axis, dim):
    if lax.axis_size(axis) != 2:
        return lax.all_gather(shard, axis, axis=dim, tiled=True)
    other = swapped(shard, axis)
    first = lax.axis_index(axis) == 0
    return jnp.concatenate(
        [jnp.where(first, shard, other), jnp.where(first, other, shard)], axis=dim
    )


def local(
    right_side,
    interface_inverse,
    coupling,
    trace_rows,
    deflation_basis,
    deflation_counts,
    coarse_inverse,
):
    source = right_side[0]
    inverse = interface_inverse[0]
    iface_rows = inverse.shape[0]
    face_rows = coupling.shape[2]
    slot_count = deflation_basis.shape[2]
    sub_count = lax.axis_size("sub")
    sub_index = lax.axis_index("sub")
    slot_ids = jnp.arange(slot_count, dtype=jnp.int32)
    basis = deflation_basis[0]
    live = (slot_ids < deflation_counts[0])[:, None]
    half_block = coarse_inverse[:, 0, :, 0, :]
    columns = gathered(half_block, "rep", 1)
    lower_gain = coupling[0, 0][:, None]
    upper_gain = coupling[0, 1][:, None]

    lower_at = trace_rows[0, 0]
    upper_at = trace_rows[0, 1]
    face_inverse = jnp.concatenate(
        [inverse[:, :face_rows], inverse[:, iface_rows - face_rows :]], axis=1
    )

    def coarse_input(defect):
        projected = lax.dot_general(
            basis, defect, (((0,), (0,)), ((), ())), preferred_element_type=jnp.float32
        )
        return jnp.where(live, projected, 0.0).astype(jnp.bfloat16)

    def coarse_of(inputs, riders):
        partial = jnp.einsum(
            "jsc,cm->jsm", columns, inputs, preferred_element_type=jnp.float32
        ).astype(jnp.bfloat16)
        partial, riders = lax.optimization_barrier((partial, riders))
        total = lax.dynamic_index_in_dim(partial, sub_index, 0, keepdims=False).astype(
            jnp.float32
        )
        for k in range(1, sub_count):
            piece = lax.dynamic_index_in_dim(partial, (sub_index + k) % sub_count, 0, keepdims=False)
            total = total + lax.ppermute(
                piece, "sub", [(i, (i + k) % sub_count) for i in range(sub_count)]
            ).astype(jnp.float32)
        return total.astype(jnp.bfloat16), riders

    pairwise = lax.axis_size("tile") == 2 and ROUNDS == 2
    tile_index = lax.axis_index("tile")
    gains = coupling[0]
    if pairwise:
        gains_high = gains.T.astype(jnp.bfloat16)
        gains_low = (gains.T - gains_high.astype(jnp.float32)).astype(jnp.bfloat16)
        gains_pair = jnp.concatenate([gains_high, gains_low], axis=1)
        peers = lax.axis_size(DUCT)
        diagonal_pairs = []
        crossing_pairs = []
        for i in range(peers):
            target = i - 1 if i % 2 == 0 else i + 1
            if 0 <= target < peers:
                diagonal_pairs.append((i, target))
            target = i - 2 if i % 2 == 0 else i + 2
            if 0 <= target < peers:
                crossing_pairs.append((i, target))

    def projection_of(mix, faces, kept):
        return (
            jnp.dot(mix, faces, preferred_element_type=jnp.float32) - kept.astype(jnp.float32)
        ).astype(jnp.bfloat16)

    def face_rows_of(gain, lower, upper):
        return jnp.concatenate(
            [gain[0][:, None] * lower, gain[1][:, None] * upper], axis=0
        ).astype(jnp.bfloat16)

    base_solve = jnp.dot(inverse, source, preferred_element_type=jnp.float32)
    local_solve = base_solve
    projected = coarse_input(local_solve.astype(jnp.bfloat16))
    if pairwise:
        width = projected.shape[1]
        got = swapped(projected, "tile")
        first = tile_index == 0
        inputs = jnp.concatenate(
            [
                jnp.where(first, projected, got[:, :width]),
                jnp.where(first, got[:, :width], projected),
            ],
            axis=0,
        )
    else:
        inputs = gathered(projected, "tile", 0)
    earlier = None
    for cycle_index in range(ROUNDS):
        coarse, (solve_now, basis_now, faces_inverse_now) = coarse_of(
            inputs, (local_solve, basis, face_inverse)
        )
        lower_basis = basis_now[lower_at]
        upper_basis = basis_now[upper_at]
        if pairwise and cycle_index == 0:
            sends = jnp.where(
                live,
                jnp.dot(basis_now.T, faces_inverse_now, preferred_element_type=jnp.float32),
                0.0,
            )
            keeps = jnp.where(
                live & live.T,
                jnp.dot(basis_now.T, basis_now, preferred_element_type=jnp.float32),
                0.0,
            )
            mine = sends.astype(jnp.bfloat16)
            kept_mix = keeps.astype(jnp.bfloat16)
        coarse = jnp.where(live, coarse, jnp.zeros((), coarse.dtype))
        correction = jnp.dot(basis, coarse, preferred_element_type=jnp.float32)
        iterate = local_solve + correction
        if cycle_index == ROUNDS - 1:
            break
        lower_trace = (
            solve_now[lower_at] + jnp.dot(lower_basis, coarse, preferred_element_type=jnp.float32)
        ).astype(jnp.bfloat16)
        upper_trace = (
            solve_now[upper_at] + jnp.dot(upper_basis, coarse, preferred_element_type=jnp.float32)
        ).astype(jnp.bfloat16)
        rows = lower_trace.shape[0]
        if pairwise:
            toward_partner = jnp.where(first, upper_trace, lower_trace)
            toward_diagonal = jnp.where(first, lower_trace, upper_trace)
            width = toward_partner.shape[1]
            kept = jnp.dot(kept_mix, coarse, preferred_element_type=jnp.float32).astype(
                jnp.bfloat16
            )
            got = swapped(
                jnp.concatenate([toward_partner, kept, mine, gains_pair], axis=1), "tile"
            )
            from_diagonal = lax.ppermute(toward_diagonal, DUCT, diagonal_pairs)
            crossing = lax.ppermute(toward_diagonal, DUCT, crossing_pairs)
            from_partner = got[:, :width]
            from_lower = jnp.where(first, from_diagonal, from_partner).astype(jnp.float32)
            from_upper = jnp.where(first, from_partner, from_diagonal).astype(jnp.float32)
            faces = face_rows_of(gains, from_lower, from_upper)
            partner_lower = jnp.where(first, upper_trace, crossing).astype(jnp.float32)
            partner_upper = jnp.where(first, crossing, lower_trace).astype(jnp.float32)
            partner_kept = got[:, width : 2 * width]
            theirs = got[:, 2 * width : 2 * width + mine.shape[1]]
            tail = got[:, 2 * width + mine.shape[1] :].astype(jnp.float32)
            pair = gains.shape[0]
            partner_gains = (tail[:, :pair] + tail[:, pair:]).T
            partner_faces = face_rows_of(partner_gains, partner_lower, partner_upper)
            own = projection_of(mine, faces, kept)
            other = projection_of(theirs, partner_faces, partner_kept)
            inputs = jnp.concatenate(
                [jnp.where(first, own, other), jnp.where(first, other, own)], axis=0
            )
        else:
            from_lower = passed_along(upper_trace, 1).astype(jnp.float32)
            from_upper = passed_along(lower_trace, -1).astype(jnp.float32)
            faces = face_rows_of(gains, from_lower, from_upper)
        change = jnp.dot(face_inverse, faces, preferred_element_type=jnp.float32)
        local_solve = base_solve + change
        if not pairwise:
            step = change if earlier is None else change - earlier
            inputs = gathered(coarse_input((step - correction).astype(jnp.bfloat16)), "tile", 0)
        earlier = change
    return iterate.astype(jnp.bfloat16)[None]


def solution(mesh):
    placed = (
        P(("group", "sub", "tile"), None, "rep"),
        P(("group", "sub", "tile"), None, None),
        P(("group", "sub", "tile"), None, None),
        P(("group", "sub", "tile"), None, None),
        P(("group", "sub", "tile"), None, None),
        P(("group", "sub", "tile")),
        P("group", "tile", "rep", "sub", None),
    )
    return jax.shard_map(
        local,
        mesh=mesh,
        in_specs=placed,
        out_specs=P(("group", "sub", "tile"), None, "rep"),
        check_vma=False,
    )
```

```python
import jax
import jax.numpy as jnp
from jax import lax
from jax.sharding import PartitionSpec as P

ROUNDS = 2
DUCT = ("sub", "tile")


def passed_along(shard, by):
    peers = lax.axis_size(DUCT)
    pairs = [(i, i + by) for i in range(peers) if 0 <= i + by < peers]
    return lax.ppermute(shard, DUCT, pairs)


def swapped(shard, axis):
    return lax.ppermute(shard, axis, [(0, 1), (1, 0)])


def gathered(shard, axis, dim):
    if lax.axis_size(axis) != 2:
        return lax.all_gather(shard, axis, axis=dim, tiled=True)
    other = swapped(shard, axis)
    first = lax.axis_index(axis) == 0
    return jnp.concatenate(
        [jnp.where(first, shard, other), jnp.where(first, other, shard)], axis=dim
    )


def local(
    right_side,
    interface_inverse,
    coupling,
    trace_rows,
    deflation_basis,
    deflation_counts,
    coarse_inverse,
):
    source = right_side[0]
    inverse = interface_inverse[0]
    iface_rows = inverse.shape[0]
    face_rows = coupling.shape[2]
    slot_count = deflation_basis.shape[2]
    sub_count = lax.axis_size("sub")
    sub_index = lax.axis_index("sub")
    slot_ids = jnp.arange(slot_count, dtype=jnp.int32)
    basis = deflation_basis[0]
    live = (slot_ids < deflation_counts[0])[:, None]
    half_block = coarse_inverse[:, 0, :, 0, :]
    columns = gathered(half_block, "rep", 1)
    lower_gain = coupling[0, 0][:, None]
    upper_gain = coupling[0, 1][:, None]

    lower_at = trace_rows[0, 0]
    upper_at = trace_rows[0, 1]
    face_inverse = jnp.concatenate(
        [inverse[:, :face_rows], inverse[:, iface_rows - face_rows :]], axis=1
    )

    def coarse_input(defect):
        projected = lax.dot_general(
            basis, defect, (((0,), (0,)), ((), ())), preferred_element_type=jnp.float32
        )
        return jnp.where(live, projected, 0.0).astype(jnp.bfloat16)

    def coarse_of(inputs, riders):
        partial = jnp.einsum(
            "jsc,cm->jsm", columns, inputs, preferred_element_type=jnp.float32
        ).astype(jnp.bfloat16)
        partial, riders = lax.optimization_barrier((partial, riders))
        total = lax.dynamic_index_in_dim(partial, sub_index, 0, keepdims=False).astype(
            jnp.float32
        )
        for k in range(1, sub_count):
            piece = lax.dynamic_index_in_dim(partial, (sub_index + k) % sub_count, 0, keepdims=False)
            total = total + lax.ppermute(
                piece, "sub", [(i, (i + k) % sub_count) for i in range(sub_count)]
            ).astype(jnp.float32)
        return total.astype(jnp.bfloat16), riders

    pairwise = lax.axis_size("tile") == 2 and ROUNDS == 2
    tile_index = lax.axis_index("tile")
    gains = coupling[0]
    if pairwise:
        gains_high = gains.T.astype(jnp.bfloat16)
        gains_low = (gains.T - gains_high.astype(jnp.float32)).astype(jnp.bfloat16)
        gains_pair = jnp.concatenate([gains_high, gains_low], axis=1)
        peers = lax.axis_size(DUCT)
        diagonal_pairs = []
        crossing_pairs = []
        for i in range(peers):
            target = i - 1 if i % 2 == 0 else i + 1
            if 0 <= target < peers:
                diagonal_pairs.append((i, target))
            target = i - 2 if i % 2 == 0 else i + 2
            if 0 <= target < peers:
                crossing_pairs.append((i, target))

    def projection_of(mix, faces, coarse):
        return (
            jnp.dot(mix[:, : faces.shape[0]], faces, preferred_element_type=jnp.float32)
            - jnp.dot(mix[:, faces.shape[0] :], coarse, preferred_element_type=jnp.float32)
        ).astype(jnp.bfloat16)

    def face_rows_of(gain, lower, upper):
        return jnp.concatenate(
            [gain[0][:, None] * lower, gain[1][:, None] * upper], axis=0
        ).astype(jnp.bfloat16)

    base_solve = jnp.dot(inverse, source, preferred_element_type=jnp.float32)
    local_solve = base_solve
    projected = coarse_input(local_solve.astype(jnp.bfloat16))
    if pairwise:
        width = projected.shape[1]
        got = swapped(projected, "tile")
        first = tile_index == 0
        inputs = jnp.concatenate(
            [
                jnp.where(first, projected, got[:, :width]),
                jnp.where(first, got[:, :width], projected),
            ],
            axis=0,
        )
    else:
        inputs = gathered(projected, "tile", 0)
    earlier = None
    for cycle_index in range(ROUNDS):
        coarse, (solve_now, basis_now, faces_inverse_now) = coarse_of(
            inputs, (local_solve, basis, face_inverse)
        )
        if pairwise:
            near_at = jnp.where(first, upper_at, lower_at)
            far_at = jnp.where(first, lower_at, upper_at)
        else:
            near_at, far_at = upper_at, lower_at
        near_basis = basis_now[near_at]
        far_basis = basis_now[far_at]
        if pairwise and cycle_index == 0:
            sends = jnp.where(
                live,
                jnp.dot(basis_now.T, faces_inverse_now, preferred_element_type=jnp.float32),
                0.0,
            )
            keeps = jnp.where(
                live & live.T,
                jnp.dot(basis_now.T, basis_now, preferred_element_type=jnp.float32),
                0.0,
            )
            mine = jnp.concatenate([sends, keeps], axis=1).astype(jnp.bfloat16)
        coarse = jnp.where(live, coarse, jnp.zeros((), coarse.dtype))
        correction = jnp.dot(basis, coarse, preferred_element_type=jnp.float32)
        iterate = local_solve + correction
        if cycle_index == ROUNDS - 1:
            break
        near_trace = (
            solve_now[near_at] + jnp.dot(near_basis, coarse, preferred_element_type=jnp.float32)
        ).astype(jnp.bfloat16)
        far_trace = (
            solve_now[far_at] + jnp.dot(far_basis, coarse, preferred_element_type=jnp.float32)
        ).astype(jnp.bfloat16)
        upper_trace, lower_trace = near_trace, far_trace
        if pairwise:
            toward_partner = near_trace
            toward_diagonal = far_trace
            width = toward_partner.shape[1]
            got = swapped(
                jnp.concatenate([toward_partner, coarse, mine, gains_pair], axis=1), "tile"
            )
            from_diagonal = lax.ppermute(toward_diagonal, DUCT, diagonal_pairs)
            crossing = lax.ppermute(toward_diagonal, DUCT, crossing_pairs)
            from_partner = got[:, :width]
            from_lower = jnp.where(first, from_diagonal, from_partner).astype(jnp.float32)
            from_upper = jnp.where(first, from_partner, from_diagonal).astype(jnp.float32)
            faces = face_rows_of(gains, from_lower, from_upper)
            partner_lower = jnp.where(first, toward_partner, crossing).astype(jnp.float32)
            partner_upper = jnp.where(first, crossing, toward_partner).astype(jnp.float32)
            partner_coarse = got[:, width : 2 * width]
            theirs = got[:, 2 * width : 2 * width + mine.shape[1]]
            tail = got[:, 2 * width + mine.shape[1] :].astype(jnp.float32)
            pair = gains.shape[0]
            partner_gains = (tail[:, :pair] + tail[:, pair:]).T
            partner_faces = face_rows_of(partner_gains, partner_lower, partner_upper)
            own = projection_of(mine, faces, coarse)
            other = projection_of(theirs, partner_faces, partner_coarse)
            inputs = jnp.concatenate(
                [jnp.where(first, own, other), jnp.where(first, other, own)], axis=0
            )
        else:
            from_lower = passed_along(upper_trace, 1).astype(jnp.float32)
            from_upper = passed_along(lower_trace, -1).astype(jnp.float32)
            faces = face_rows_of(gains, from_lower, from_upper)
        change = jnp.dot(face_inverse, faces, preferred_element_type=jnp.float32)
        local_solve = base_solve + change
        if not pairwise:
            step = change if earlier is None else change - earlier
            inputs = gathered(coarse_input((step - correction).astype(jnp.bfloat16)), "tile", 0)
        earlier = change
    return iterate.astype(jnp.bfloat16)[None]


def solution(mesh):
    placed = (
        P(("group", "sub", "tile"), None, "rep"),
        P(("group", "sub", "tile"), None, None),
        P(("group", "sub", "tile"), None, None),
        P(("group", "sub", "tile"), None, None),
        P(("group", "sub", "tile"), None, None),
        P(("group", "sub", "tile")),
        P("group", "tile", "rep", "sub", None),
    )
    return jax.shard_map(
        local,
        mesh=mesh,
        in_specs=placed,
        out_specs=P(("group", "sub", "tile"), None, "rep"),
        check_vma=False,
    )
```

```python
import jax
import jax.numpy as jnp
from jax import lax
from jax.sharding import PartitionSpec as P

ROUNDS = 2
DUCT = ("sub", "tile")


def passed_along(shard, by):
    peers = lax.axis_size(DUCT)
    pairs = [(i, i + by) for i in range(peers) if 0 <= i + by < peers]
    return lax.ppermute(shard, DUCT, pairs)


def swapped(shard, axis):
    return lax.ppermute(shard, axis, [(0, 1), (1, 0)])


def gathered(shard, axis, dim):
    if lax.axis_size(axis) != 2:
        return lax.all_gather(shard, axis, axis=dim, tiled=True)
    other = swapped(shard, axis)
    first = lax.axis_index(axis) == 0
    return jnp.concatenate(
        [jnp.where(first, shard, other), jnp.where(first, other, shard)], axis=dim
    )


def local(
    right_side,
    interface_inverse,
    coupling,
    trace_rows,
    deflation_basis,
    deflation_counts,
    coarse_inverse,
):
    source = right_side[0]
    inverse = interface_inverse[0]
    iface_rows = inverse.shape[0]
    face_rows = coupling.shape[2]
    slot_count = deflation_basis.shape[2]
    sub_count = lax.axis_size("sub")
    sub_index = lax.axis_index("sub")
    slot_ids = jnp.arange(slot_count, dtype=jnp.int32)
    basis = deflation_basis[0]
    live = (slot_ids < deflation_counts[0])[:, None]
    half_block = coarse_inverse[:, 0, :, 0, :]
    columns = gathered(half_block, "rep", 1)
    lower_gain = coupling[0, 0][:, None]
    upper_gain = coupling[0, 1][:, None]

    lower_at = trace_rows[0, 0]
    upper_at = trace_rows[0, 1]
    face_inverse = jnp.concatenate(
        [inverse[:, :face_rows], inverse[:, iface_rows - face_rows :]], axis=1
    )

    def coarse_input(defect):
        projected = lax.dot_general(
            basis, defect, (((0,), (0,)), ((), ())), preferred_element_type=jnp.float32
        )
        return jnp.where(live, projected, 0.0).astype(jnp.bfloat16)

    def coarse_of(inputs, riders):
        partial = jnp.einsum(
            "jsc,cm->jsm", columns, inputs, preferred_element_type=jnp.float32
        ).astype(jnp.bfloat16)
        partial, riders = lax.optimization_barrier((partial, riders))
        total = lax.dynamic_index_in_dim(partial, sub_index, 0, keepdims=False).astype(
            jnp.float32
        )
        paired = sub_count & (sub_count - 1) == 0
        for k in range(1, sub_count):
            if paired:
                target = sub_index ^ k
                pairs = [(i, i ^ k) for i in range(sub_count)]
            else:
                target = (sub_index + k) % sub_count
                pairs = [(i, (i + k) % sub_count) for i in range(sub_count)]
            piece = lax.dynamic_index_in_dim(partial, target, 0, keepdims=False)
            total = total + lax.ppermute(piece, "sub", pairs).astype(jnp.float32)
        return total.astype(jnp.bfloat16), riders

    pairwise = lax.axis_size("tile") == 2 and ROUNDS == 2
    tile_index = lax.axis_index("tile")
    gains = coupling[0]
    if pairwise:
        gains_high = gains.T.astype(jnp.bfloat16)
        gains_low = (gains.T - gains_high.astype(jnp.float32)).astype(jnp.bfloat16)
        gains_pair = jnp.concatenate([gains_high, gains_low], axis=1)
        peers = lax.axis_size(DUCT)
        diagonal_pairs = []
        crossing_pairs = []
        for i in range(peers):
            target = i - 1 if i % 2 == 0 else i + 1
            if 0 <= target < peers:
                diagonal_pairs.append((i, target))
            target = i - 2 if i % 2 == 0 else i + 2
            if 0 <= target < peers:
                crossing_pairs.append((i, target))

    def projection_of(mix, faces, coarse):
        return (
            jnp.dot(mix[:, : faces.shape[0]], faces, preferred_element_type=jnp.float32)
            - jnp.dot(mix[:, faces.shape[0] :], coarse, preferred_element_type=jnp.float32)
        ).astype(jnp.bfloat16)

    def face_rows_of(gain, lower, upper):
        return jnp.concatenate(
            [gain[0][:, None] * lower, gain[1][:, None] * upper], axis=0
        ).astype(jnp.bfloat16)

    base_solve = jnp.dot(inverse, source, preferred_element_type=jnp.float32)
    local_solve = base_solve
    projected = coarse_input(local_solve.astype(jnp.bfloat16))
    if pairwise:
        width = projected.shape[1]
        got = swapped(projected, "tile")
        first = tile_index == 0
        inputs = jnp.concatenate(
            [
                jnp.where(first, projected, got[:, :width]),
                jnp.where(first, got[:, :width], projected),
            ],
            axis=0,
        )
    else:
        inputs = gathered(projected, "tile", 0)
    earlier = None
    for cycle_index in range(ROUNDS):
        coarse, (solve_now, basis_now, faces_inverse_now) = coarse_of(
            inputs, (local_solve, basis, face_inverse)
        )
        lower_basis = basis_now[lower_at]
        upper_basis = basis_now[upper_at]
        if pairwise and cycle_index == 0:
            sends = jnp.where(
                live,
                jnp.dot(basis_now.T, faces_inverse_now, preferred_element_type=jnp.float32),
                0.0,
            )
            keeps = jnp.where(
                live & live.T,
                jnp.dot(basis_now.T, basis_now, preferred_element_type=jnp.float32),
                0.0,
            )
            mine = jnp.concatenate([sends, keeps], axis=1).astype(jnp.bfloat16)
        coarse = jnp.where(live, coarse, jnp.zeros((), coarse.dtype))
        correction = jnp.dot(basis, coarse, preferred_element_type=jnp.float32)
        iterate = local_solve + correction
        if cycle_index == ROUNDS - 1:
            break
        lower_trace = (
            solve_now[lower_at] + jnp.dot(lower_basis, coarse, preferred_element_type=jnp.float32)
        ).astype(jnp.bfloat16)
        upper_trace = (
            solve_now[upper_at] + jnp.dot(upper_basis, coarse, preferred_element_type=jnp.float32)
        ).astype(jnp.bfloat16)
        rows = lower_trace.shape[0]
        if pairwise:
            toward_partner = jnp.where(first, upper_trace, lower_trace)
            toward_diagonal = jnp.where(first, lower_trace, upper_trace)
            width = toward_partner.shape[1]
            got = swapped(
                jnp.concatenate([toward_partner, coarse, mine, gains_pair], axis=1), "tile"
            )
            from_diagonal = lax.ppermute(toward_diagonal, DUCT, diagonal_pairs)
            crossing = lax.ppermute(toward_diagonal, DUCT, crossing_pairs)
            from_partner = got[:, :width]
            from_lower = jnp.where(first, from_diagonal, from_partner).astype(jnp.float32)
            from_upper = jnp.where(first, from_partner, from_diagonal).astype(jnp.float32)
            faces = face_rows_of(gains, from_lower, from_upper)
            partner_lower = jnp.where(first, upper_trace, crossing).astype(jnp.float32)
            partner_upper = jnp.where(first, crossing, lower_trace).astype(jnp.float32)
            partner_coarse = got[:, width : 2 * width]
            theirs = got[:, 2 * width : 2 * width + mine.shape[1]]
            tail = got[:, 2 * width + mine.shape[1] :].astype(jnp.float32)
            pair = gains.shape[0]
            partner_gains = (tail[:, :pair] + tail[:, pair:]).T
            partner_faces = face_rows_of(partner_gains, partner_lower, partner_upper)
            own = projection_of(mine, faces, coarse)
            other = projection_of(theirs, partner_faces, partner_coarse)
            inputs = jnp.concatenate(
                [jnp.where(first, own, other), jnp.where(first, other, own)], axis=0
            )
        else:
            from_lower = passed_along(upper_trace, 1).astype(jnp.float32)
            from_upper = passed_along(lower_trace, -1).astype(jnp.float32)
            faces = face_rows_of(gains, from_lower, from_upper)
        change = jnp.dot(face_inverse, faces, preferred_element_type=jnp.float32)
        local_solve = base_solve + change
        if not pairwise:
            step = change if earlier is None else change - earlier
            inputs = gathered(coarse_input((step - correction).astype(jnp.bfloat16)), "tile", 0)
        earlier = change
    return iterate.astype(jnp.bfloat16)[None]


def solution(mesh):
    placed = (
        P(("group", "sub", "tile"), None, "rep"),
        P(("group", "sub", "tile"), None, None),
        P(("group", "sub", "tile"), None, None),
        P(("group", "sub", "tile"), None, None),
        P(("group", "sub", "tile"), None, None),
        P(("group", "sub", "tile")),
        P("group", "tile", "rep", "sub", None),
    )
    return jax.shard_map(
        local,
        mesh=mesh,
        in_specs=placed,
        out_specs=P(("group", "sub", "tile"), None, "rep"),
        check_vma=False,
    )
```

```python
import jax
import jax.numpy as jnp
from jax import lax
from jax.sharding import PartitionSpec as P

ROUNDS = 2
DUCT = ("sub", "tile")


def passed_along(shard, by):
    peers = lax.axis_size(DUCT)
    pairs = [(i, i + by) for i in range(peers) if 0 <= i + by < peers]
    return lax.ppermute(shard, DUCT, pairs)


def swapped(shard, axis):
    return lax.ppermute(shard, axis, [(0, 1), (1, 0)])


def gathered(shard, axis, dim):
    if lax.axis_size(axis) != 2:
        return lax.all_gather(shard, axis, axis=dim, tiled=True)
    other = swapped(shard, axis)
    first = lax.axis_index(axis) == 0
    return jnp.concatenate(
        [jnp.where(first, shard, other), jnp.where(first, other, shard)], axis=dim
    )


def local(
    right_side,
    interface_inverse,
    coupling,
    trace_rows,
    deflation_basis,
    deflation_counts,
    coarse_inverse,
):
    source = right_side[0]
    inverse = interface_inverse[0]
    iface_rows = inverse.shape[0]
    face_rows = coupling.shape[2]
    slot_count = deflation_basis.shape[2]
    sub_count = lax.axis_size("sub")
    sub_index = lax.axis_index("sub")
    slot_ids = jnp.arange(slot_count, dtype=jnp.int32)
    basis = deflation_basis[0]
    live = (slot_ids < deflation_counts[0])[:, None]
    half_block = coarse_inverse[:, 0, :, 0, :]
    columns = gathered(half_block, "rep", 1)
    lower_gain = coupling[0, 0][:, None]
    upper_gain = coupling[0, 1][:, None]

    lower_at = trace_rows[0, 0]
    upper_at = trace_rows[0, 1]
    face_inverse = jnp.concatenate(
        [inverse[:, :face_rows], inverse[:, iface_rows - face_rows :]], axis=1
    )

    def coarse_input(defect):
        projected = lax.dot_general(
            basis, defect, (((0,), (0,)), ((), ())), preferred_element_type=jnp.float32
        )
        return jnp.where(live, projected, 0.0).astype(jnp.bfloat16)

    def coarse_of(inputs, riders):
        partial = jnp.einsum(
            "jsc,cm->jsm", columns, inputs, preferred_element_type=jnp.float32
        ).astype(jnp.bfloat16)
        partial, riders = lax.optimization_barrier((partial, riders))
        total = lax.dynamic_index_in_dim(partial, sub_index, 0, keepdims=False).astype(
            jnp.float32
        )
        for k in range(1, sub_count):
            piece = lax.dynamic_index_in_dim(partial, (sub_index + k) % sub_count, 0, keepdims=False)
            total = total + lax.ppermute(
                piece, "sub", [(i, (i + k) % sub_count) for i in range(sub_count)]
            ).astype(jnp.float32)
        return total.astype(jnp.bfloat16), riders

    pairwise = lax.axis_size("tile") == 2 and ROUNDS == 2
    tile_index = lax.axis_index("tile")
    gains = coupling[0]
    if pairwise:
        gains_high = gains.T.astype(jnp.bfloat16)
        gains_low = (gains.T - gains_high.astype(jnp.float32)).astype(jnp.bfloat16)
        gains_pair = jnp.concatenate([gains_high, gains_low], axis=1)
        peers = lax.axis_size(DUCT)
        diagonal_pairs = []
        crossing_pairs = []
        for i in range(peers):
            target = i - 1 if i % 2 == 0 else i + 1
            if 0 <= target < peers:
                diagonal_pairs.append((i, target))
            target = i - 2 if i % 2 == 0 else i + 2
            if 0 <= target < peers:
                crossing_pairs.append((i, target))

    def projection_of(mix, faces, coarse):
        return (
            jnp.dot(mix[:, : faces.shape[0]], faces, preferred_element_type=jnp.float32)
            - jnp.dot(mix[:, faces.shape[0] :], coarse, preferred_element_type=jnp.float32)
        ).astype(jnp.bfloat16)

    def face_rows_of(gain, lower, upper):
        return jnp.concatenate(
            [gain[0][:, None] * lower, gain[1][:, None] * upper], axis=0
        ).astype(jnp.bfloat16)

    base_solve = jnp.dot(inverse, source, preferred_element_type=jnp.float32)
    local_solve = base_solve
    projected = coarse_input(local_solve.astype(jnp.bfloat16))
    if pairwise:
        width = projected.shape[1]
        got = swapped(projected, "tile")
        first = tile_index == 0
        inputs = jnp.concatenate(
            [
                jnp.where(first, projected, got[:, :width]),
                jnp.where(first, got[:, :width], projected),
            ],
            axis=0,
        )
    else:
        inputs = gathered(projected, "tile", 0)
    earlier = None
    for cycle_index in range(ROUNDS):
        coarse, (solve_now, basis_now, faces_inverse_now) = coarse_of(
            inputs, (local_solve, basis, face_inverse)
        )
        lower_basis = basis_now[lower_at]
        upper_basis = basis_now[upper_at]
        if pairwise and cycle_index == 0:
            sends = jnp.where(
                live,
                jnp.dot(basis_now.T, faces_inverse_now, preferred_element_type=jnp.float32),
                0.0,
            )
            keeps = jnp.where(
                live & live.T,
                jnp.dot(basis_now.T, basis_now, preferred_element_type=jnp.float32),
                0.0,
            )
            mine = jnp.concatenate([sends, keeps], axis=1).astype(jnp.bfloat16)
        coarse = jnp.where(live, coarse, jnp.zeros((), coarse.dtype))
        correction = jnp.dot(basis, coarse, preferred_element_type=jnp.float32)
        iterate = solve_now + correction
        if cycle_index == ROUNDS - 1:
            break
        lower_trace = (
            solve_now[lower_at] + jnp.dot(lower_basis, coarse, preferred_element_type=jnp.float32)
        ).astype(jnp.bfloat16)
        upper_trace = (
            solve_now[upper_at] + jnp.dot(upper_basis, coarse, preferred_element_type=jnp.float32)
        ).astype(jnp.bfloat16)
        rows = lower_trace.shape[0]
        if pairwise:
            toward_partner = jnp.where(first, upper_trace, lower_trace)
            toward_diagonal = jnp.where(first, lower_trace, upper_trace)
            width = toward_partner.shape[1]
            got = swapped(
                jnp.concatenate([toward_partner, coarse, mine, gains_pair], axis=1), "tile"
            )
            from_diagonal = lax.ppermute(toward_diagonal, DUCT, diagonal_pairs)
            crossing = lax.ppermute(toward_diagonal, DUCT, crossing_pairs)
            from_partner = got[:, :width]
            from_lower = jnp.where(first, from_diagonal, from_partner).astype(jnp.float32)
            from_upper = jnp.where(first, from_partner, from_diagonal).astype(jnp.float32)
            faces = face_rows_of(gains, from_lower, from_upper)
            partner_lower = jnp.where(first, upper_trace, crossing).astype(jnp.float32)
            partner_upper = jnp.where(first, crossing, lower_trace).astype(jnp.float32)
            partner_coarse = got[:, width : 2 * width]
            theirs = got[:, 2 * width : 2 * width + mine.shape[1]]
            tail = got[:, 2 * width + mine.shape[1] :].astype(jnp.float32)
            pair = gains.shape[0]
            partner_gains = (tail[:, :pair] + tail[:, pair:]).T
            partner_faces = face_rows_of(partner_gains, partner_lower, partner_upper)
            own = projection_of(mine, faces, coarse)
            other = projection_of(theirs, partner_faces, partner_coarse)
            inputs = jnp.concatenate(
                [jnp.where(first, own, other), jnp.where(first, other, own)], axis=0
            )
        else:
            from_lower = passed_along(upper_trace, 1).astype(jnp.float32)
            from_upper = passed_along(lower_trace, -1).astype(jnp.float32)
            faces = face_rows_of(gains, from_lower, from_upper)
        change = jnp.dot(face_inverse, faces, preferred_element_type=jnp.float32)
        local_solve = base_solve + change
        if not pairwise:
            step = change if earlier is None else change - earlier
            inputs = gathered(coarse_input((step - correction).astype(jnp.bfloat16)), "tile", 0)
        earlier = change
    return iterate.astype(jnp.bfloat16)[None]


def solution(mesh):
    placed = (
        P(("group", "sub", "tile"), None, "rep"),
        P(("group", "sub", "tile"), None, None),
        P(("group", "sub", "tile"), None, None),
        P(("group", "sub", "tile"), None, None),
        P(("group", "sub", "tile"), None, None),
        P(("group", "sub", "tile")),
        P("group", "tile", "rep", "sub", None),
    )
    return jax.shard_map(
        local,
        mesh=mesh,
        in_specs=placed,
        out_specs=P(("group", "sub", "tile"), None, "rep"),
        check_vma=False,
    )
```

```python
import jax
import jax.numpy as jnp
from jax import lax
from jax.sharding import PartitionSpec as P

ROUNDS = 2
DUCT = ("sub", "tile")


def passed_along(shard, by):
    peers = lax.axis_size(DUCT)
    pairs = [(i, i + by) for i in range(peers) if 0 <= i + by < peers]
    return lax.ppermute(shard, DUCT, pairs)


def swapped(shard, axis):
    return lax.ppermute(shard, axis, [(0, 1), (1, 0)])


def gathered(shard, axis, dim):
    if lax.axis_size(axis) != 2:
        return lax.all_gather(shard, axis, axis=dim, tiled=True)
    other = swapped(shard, axis)
    first = lax.axis_index(axis) == 0
    return jnp.concatenate(
        [jnp.where(first, shard, other), jnp.where(first, other, shard)], axis=dim
    )


def local(
    right_side,
    interface_inverse,
    coupling,
    trace_rows,
    deflation_basis,
    deflation_counts,
    coarse_inverse,
):
    source = right_side[0]
    inverse = interface_inverse[0]
    iface_rows = inverse.shape[0]
    face_rows = coupling.shape[2]
    slot_count = deflation_basis.shape[2]
    sub_count = lax.axis_size("sub")
    sub_index = lax.axis_index("sub")
    slot_ids = jnp.arange(slot_count, dtype=jnp.int32)
    basis = deflation_basis[0]
    live = (slot_ids < deflation_counts[0])[:, None]
    half_block = coarse_inverse[:, 0, :, 0, :]
    columns = gathered(half_block, "rep", 1)
    lower_gain = coupling[0, 0][:, None]
    upper_gain = coupling[0, 1][:, None]

    lower_at = trace_rows[0, 0]
    upper_at = trace_rows[0, 1]
    face_inverse = jnp.concatenate(
        [inverse[:, :face_rows], inverse[:, iface_rows - face_rows :]], axis=1
    )

    def coarse_input(defect):
        projected = lax.dot_general(
            basis, defect, (((0,), (0,)), ((), ())), preferred_element_type=jnp.float32
        )
        return jnp.where(live, projected, 0.0).astype(jnp.bfloat16)

    def coarse_of(inputs, riders):
        partial = jnp.einsum(
            "jsc,cm->jsm", columns, inputs, preferred_element_type=jnp.float32
        ).astype(jnp.bfloat16)
        partial, riders = lax.optimization_barrier((partial, riders))
        total = lax.dynamic_index_in_dim(partial, sub_index, 0, keepdims=False).astype(
            jnp.float32
        )
        for k in range(1, sub_count):
            piece = lax.dynamic_index_in_dim(partial, (sub_index + k) % sub_count, 0, keepdims=False)
            total = total + lax.ppermute(
                piece, "sub", [(i, (i + k) % sub_count) for i in range(sub_count)]
            ).astype(jnp.float32)
        return total.astype(jnp.bfloat16), riders

    pairwise = lax.axis_size("tile") == 2 and ROUNDS == 2
    tile_index = lax.axis_index("tile")
    gains = coupling[0]
    if pairwise:
        gains_high = gains.T.astype(jnp.bfloat16)
        gains_low = (gains.T - gains_high.astype(jnp.float32)).astype(jnp.bfloat16)
        gains_pair = jnp.concatenate([gains_high, gains_low], axis=1)
        peers = lax.axis_size(DUCT)
        diagonal_pairs = []
        crossing_pairs = []
        for i in range(peers):
            target = i - 1 if i % 2 == 0 else i + 1
            if 0 <= target < peers:
                diagonal_pairs.append((i, target))
            target = i - 2 if i % 2 == 0 else i + 2
            if 0 <= target < peers:
                crossing_pairs.append((i, target))

    def projection_of(mix, faces, coarse):
        return (
            jnp.dot(mix[:, : faces.shape[0]], faces, preferred_element_type=jnp.float32)
            - jnp.dot(mix[:, faces.shape[0] :], coarse, preferred_element_type=jnp.float32)
        ).astype(jnp.bfloat16)

    def face_rows_of(gain, lower, upper):
        return jnp.concatenate(
            [gain[0][:, None] * lower, gain[1][:, None] * upper], axis=0
        ).astype(jnp.bfloat16)

    base_solve = jnp.dot(inverse, source, preferred_element_type=jnp.float32)
    local_solve = base_solve
    projected = coarse_input(local_solve.astype(jnp.bfloat16))
    row_basis, _ = lax.optimization_barrier((basis, projected))
    lower_basis = row_basis[lower_at]
    upper_basis = row_basis[upper_at]
    if pairwise:
        width = projected.shape[1]
        got = swapped(projected, "tile")
        first = tile_index == 0
        inputs = jnp.concatenate(
            [
                jnp.where(first, projected, got[:, :width]),
                jnp.where(first, got[:, :width], projected),
            ],
            axis=0,
        )
    else:
        inputs = gathered(projected, "tile", 0)
    earlier = None
    for cycle_index in range(ROUNDS):
        coarse, (solve_now, basis_now, faces_inverse_now) = coarse_of(
            inputs, (local_solve, basis, face_inverse)
        )
        if pairwise and cycle_index == 0:
            sends = jnp.where(
                live,
                jnp.dot(basis_now.T, faces_inverse_now, preferred_element_type=jnp.float32),
                0.0,
            )
            keeps = jnp.where(
                live & live.T,
                jnp.dot(basis_now.T, basis_now, preferred_element_type=jnp.float32),
                0.0,
            )
            mine = jnp.concatenate([sends, keeps], axis=1).astype(jnp.bfloat16)
        coarse = jnp.where(live, coarse, jnp.zeros((), coarse.dtype))
        correction = jnp.dot(basis, coarse, preferred_element_type=jnp.float32)
        iterate = local_solve + correction
        if cycle_index == ROUNDS - 1:
            break
        lower_trace = (
            solve_now[lower_at] + jnp.dot(lower_basis, coarse, preferred_element_type=jnp.float32)
        ).astype(jnp.bfloat16)
        upper_trace = (
            solve_now[upper_at] + jnp.dot(upper_basis, coarse, preferred_element_type=jnp.float32)
        ).astype(jnp.bfloat16)
        rows = lower_trace.shape[0]
        if pairwise:
            toward_partner = jnp.where(first, upper_trace, lower_trace)
            toward_diagonal = jnp.where(first, lower_trace, upper_trace)
            width = toward_partner.shape[1]
            got = swapped(
                jnp.concatenate([toward_partner, coarse, mine, gains_pair], axis=1), "tile"
            )
            from_diagonal = lax.ppermute(toward_diagonal, DUCT, diagonal_pairs)
            crossing = lax.ppermute(toward_diagonal, DUCT, crossing_pairs)
            from_partner = got[:, :width]
            from_lower = jnp.where(first, from_diagonal, from_partner).astype(jnp.float32)
            from_upper = jnp.where(first, from_partner, from_diagonal).astype(jnp.float32)
            faces = face_rows_of(gains, from_lower, from_upper)
            partner_lower = jnp.where(first, upper_trace, crossing).astype(jnp.float32)
            partner_upper = jnp.where(first, crossing, lower_trace).astype(jnp.float32)
            partner_coarse = got[:, width : 2 * width]
            theirs = got[:, 2 * width : 2 * width + mine.shape[1]]
            tail = got[:, 2 * width + mine.shape[1] :].astype(jnp.float32)
            pair = gains.shape[0]
            partner_gains = (tail[:, :pair] + tail[:, pair:]).T
            partner_faces = face_rows_of(partner_gains, partner_lower, partner_upper)
            own = projection_of(mine, faces, coarse)
            other = projection_of(theirs, partner_faces, partner_coarse)
            inputs = jnp.concatenate(
                [jnp.where(first, own, other), jnp.where(first, other, own)], axis=0
            )
        else:
            from_lower = passed_along(upper_trace, 1).astype(jnp.float32)
            from_upper = passed_along(lower_trace, -1).astype(jnp.float32)
            faces = face_rows_of(gains, from_lower, from_upper)
        change = jnp.dot(face_inverse, faces, preferred_element_type=jnp.float32)
        local_solve = base_solve + change
        if not pairwise:
            step = change if earlier is None else change - earlier
            inputs = gathered(coarse_input((step - correction).astype(jnp.bfloat16)), "tile", 0)
        earlier = change
    return iterate.astype(jnp.bfloat16)[None]


def solution(mesh):
    placed = (
        P(("group", "sub", "tile"), None, "rep"),
        P(("group", "sub", "tile"), None, None),
        P(("group", "sub", "tile"), None, None),
        P(("group", "sub", "tile"), None, None),
        P(("group", "sub", "tile"), None, None),
        P(("group", "sub", "tile")),
        P("group", "tile", "rep", "sub", None),
    )
    return jax.shard_map(
        local,
        mesh=mesh,
        in_specs=placed,
        out_specs=P(("group", "sub", "tile"), None, "rep"),
        check_vma=False,
    )
```

```python
import jax
import jax.numpy as jnp
from jax import lax
from jax.sharding import PartitionSpec as P

ROUNDS = 2
DUCT = ("sub", "tile")


def passed_along(shard, by):
    peers = lax.axis_size(DUCT)
    pairs = [(i, i + by) for i in range(peers) if 0 <= i + by < peers]
    return lax.ppermute(shard, DUCT, pairs)


def swapped(shard, axis):
    return lax.ppermute(shard, axis, [(0, 1), (1, 0)])


def gathered(shard, axis, dim):
    if lax.axis_size(axis) != 2:
        return lax.all_gather(shard, axis, axis=dim, tiled=True)
    other = swapped(shard, axis)
    first = lax.axis_index(axis) == 0
    return jnp.concatenate(
        [jnp.where(first, shard, other), jnp.where(first, other, shard)], axis=dim
    )


def local(
    right_side,
    interface_inverse,
    coupling,
    trace_rows,
    deflation_basis,
    deflation_counts,
    coarse_inverse,
):
    source = right_side[0]
    inverse = interface_inverse[0]
    iface_rows = inverse.shape[0]
    face_rows = coupling.shape[2]
    slot_count = deflation_basis.shape[2]
    sub_count = lax.axis_size("sub")
    sub_index = lax.axis_index("sub")
    slot_ids = jnp.arange(slot_count, dtype=jnp.int32)
    basis = deflation_basis[0]
    live = (slot_ids < deflation_counts[0])[:, None]
    half_block = coarse_inverse[:, 0, :, 0, :]
    columns = gathered(half_block, "rep", 1)
    lower_gain = coupling[0, 0][:, None]
    upper_gain = coupling[0, 1][:, None]

    lower_at = trace_rows[0, 0]
    upper_at = trace_rows[0, 1]
    face_inverse = jnp.concatenate(
        [inverse[:, :face_rows], inverse[:, iface_rows - face_rows :]], axis=1
    )

    def coarse_input(defect):
        projected = lax.dot_general(
            basis, defect, (((0,), (0,)), ((), ())), preferred_element_type=jnp.float32
        )
        return jnp.where(live, projected, 0.0).astype(jnp.bfloat16)

    def coarse_of(inputs, riders):
        partial = jnp.einsum(
            "jsc,cm->jsm", columns, inputs, preferred_element_type=jnp.float32
        ).astype(jnp.bfloat16)
        partial, riders = lax.optimization_barrier((partial, riders))
        total = lax.dynamic_index_in_dim(partial, sub_index, 0, keepdims=False).astype(
            jnp.float32
        )
        half_way = sub_count // 2
        for k in [half_way] + [k for k in range(1, sub_count) if k != half_way]:
            piece = lax.dynamic_index_in_dim(partial, (sub_index + k) % sub_count, 0, keepdims=False)
            total = total + lax.ppermute(
                piece, "sub", [(i, (i + k) % sub_count) for i in range(sub_count)]
            ).astype(jnp.float32)
        return total.astype(jnp.bfloat16), riders

    pairwise = lax.axis_size("tile") == 2 and ROUNDS == 2
    tile_index = lax.axis_index("tile")
    gains = coupling[0]
    if pairwise:
        gains_high = gains.T.astype(jnp.bfloat16)
        gains_low = (gains.T - gains_high.astype(jnp.float32)).astype(jnp.bfloat16)
        gains_pair = jnp.concatenate([gains_high, gains_low], axis=1)
        peers = lax.axis_size(DUCT)
        diagonal_pairs = []
        crossing_pairs = []
        for i in range(peers):
            target = i - 1 if i % 2 == 0 else i + 1
            if 0 <= target < peers:
                diagonal_pairs.append((i, target))
            target = i - 2 if i % 2 == 0 else i + 2
            if 0 <= target < peers:
                crossing_pairs.append((i, target))

    def projection_of(mix, faces, coarse):
        return (
            jnp.dot(mix[:, : faces.shape[0]], faces, preferred_element_type=jnp.float32)
            - jnp.dot(mix[:, faces.shape[0] :], coarse, preferred_element_type=jnp.float32)
        ).astype(jnp.bfloat16)

    def face_rows_of(gain, lower, upper):
        return jnp.concatenate(
            [gain[0][:, None] * lower, gain[1][:, None] * upper], axis=0
        ).astype(jnp.bfloat16)

    base_solve = jnp.dot(inverse, source, preferred_element_type=jnp.float32)
    local_solve = base_solve
    projected = coarse_input(local_solve.astype(jnp.bfloat16))
    if pairwise:
        width = projected.shape[1]
        got = swapped(projected, "tile")
        first = tile_index == 0
        inputs = jnp.concatenate(
            [
                jnp.where(first, projected, got[:, :width]),
                jnp.where(first, got[:, :width], projected),
            ],
            axis=0,
        )
    else:
        inputs = gathered(projected, "tile", 0)
    earlier = None
    for cycle_index in range(ROUNDS):
        coarse, (solve_now, basis_now, faces_inverse_now) = coarse_of(
            inputs, (local_solve, basis, face_inverse)
        )
        lower_basis = basis_now[lower_at]
        upper_basis = basis_now[upper_at]
        if pairwise and cycle_index == 0:
            sends = jnp.where(
                live,
                jnp.dot(basis_now.T, faces_inverse_now, preferred_element_type=jnp.float32),
                0.0,
            )
            keeps = jnp.where(
                live & live.T,
                jnp.dot(basis_now.T, basis_now, preferred_element_type=jnp.float32),
                0.0,
            )
            mine = jnp.concatenate([sends, keeps], axis=1).astype(jnp.bfloat16)
        coarse = jnp.where(live, coarse, jnp.zeros((), coarse.dtype))
        correction = jnp.dot(basis, coarse, preferred_element_type=jnp.float32)
        iterate = local_solve + correction
        if cycle_index == ROUNDS - 1:
            break
        lower_trace = (
            solve_now[lower_at] + jnp.dot(lower_basis, coarse, preferred_element_type=jnp.float32)
        ).astype(jnp.bfloat16)
        upper_trace = (
            solve_now[upper_at] + jnp.dot(upper_basis, coarse, preferred_element_type=jnp.float32)
        ).astype(jnp.bfloat16)
        rows = lower_trace.shape[0]
        if pairwise:
            toward_partner = jnp.where(first, upper_trace, lower_trace)
            toward_diagonal = jnp.where(first, lower_trace, upper_trace)
            width = toward_partner.shape[1]
            got = swapped(
                jnp.concatenate([toward_partner, coarse, mine, gains_pair], axis=1), "tile"
            )
            from_diagonal = lax.ppermute(toward_diagonal, DUCT, diagonal_pairs)
            crossing = lax.ppermute(toward_diagonal, DUCT, crossing_pairs)
            from_partner = got[:, :width]
            from_lower = jnp.where(first, from_diagonal, from_partner).astype(jnp.float32)
            from_upper = jnp.where(first, from_partner, from_diagonal).astype(jnp.float32)
            faces = face_rows_of(gains, from_lower, from_upper)
            partner_lower = jnp.where(first, upper_trace, crossing).astype(jnp.float32)
            partner_upper = jnp.where(first, crossing, lower_trace).astype(jnp.float32)
            partner_coarse = got[:, width : 2 * width]
            theirs = got[:, 2 * width : 2 * width + mine.shape[1]]
            tail = got[:, 2 * width + mine.shape[1] :].astype(jnp.float32)
            pair = gains.shape[0]
            partner_gains = (tail[:, :pair] + tail[:, pair:]).T
            partner_faces = face_rows_of(partner_gains, partner_lower, partner_upper)
            own = projection_of(mine, faces, coarse)
            other = projection_of(theirs, partner_faces, partner_coarse)
            inputs = jnp.concatenate(
                [jnp.where(first, own, other), jnp.where(first, other, own)], axis=0
            )
        else:
            from_lower = passed_along(upper_trace, 1).astype(jnp.float32)
            from_upper = passed_along(lower_trace, -1).astype(jnp.float32)
            faces = face_rows_of(gains, from_lower, from_upper)
        change = jnp.dot(face_inverse, faces, preferred_element_type=jnp.float32)
        local_solve = base_solve + change
        if not pairwise:
            step = change if earlier is None else change - earlier
            inputs = gathered(coarse_input((step - correction).astype(jnp.bfloat16)), "tile", 0)
        earlier = change
    return iterate.astype(jnp.bfloat16)[None]


def solution(mesh):
    placed = (
        P(("group", "sub", "tile"), None, "rep"),
        P(("group", "sub", "tile"), None, None),
        P(("group", "sub", "tile"), None, None),
        P(("group", "sub", "tile"), None, None),
        P(("group", "sub", "tile"), None, None),
        P(("group", "sub", "tile")),
        P("group", "tile", "rep", "sub", None),
    )
    return jax.shard_map(
        local,
        mesh=mesh,
        in_specs=placed,
        out_specs=P(("group", "sub", "tile"), None, "rep"),
        check_vma=False,
    )
```
